256 devices in a mesh: layer: 32 (over z, y), plane: 8 (over x, core).
Axes of the slice: x: 4, y: 4, z: 8, core: 2. Of those that a mesh axis runs over, the one named last changes fastest.
Arguments:
- rhs_field: float32 [32, 2, 4, 64, 1024], P('layer', None, None, None, 'plane'), may hold values from -6 to 6
- panel_inverse: bfloat16 [32, 1024, 2048], P('layer'), may hold values from -1 to 1
- coupling: float32 [32, 2, 4, 64], P('layer', None, None, 'plane'), may hold values from -0.98 to 0.98, as said below
Outputs:
- sweep_field: float32 [32, 2, 4, 64, 1024], P('layer', None, None, None, 'plane')
The draws below stay inside these ranges and needn't reach their ends.
Inputs may be any that keep to these rules, and one draw needn't show every extreme that they name: Every complex coupling has modulus at most 0.98.
All inputs are finite; a program needn't handle non-finite values.
Results may differ from the reference program's by a relative error of at most 0.025.
Values may be sent and summed in bfloat16 or wider, within the bound.
No kernel may reach another device: no remote copies, remote signals or barrier semaphores. Data moves between devices by JAX's collectives and lax.ppermute only.
A program may use at most 64 MiB of HBM per device.

```python
import math
import jax
import jax.numpy as jnp
from jax import lax

NX = 1024
LOAD_VECTORS = 4
LATERAL_POINTS = 64
DEPTH_SLABS = 32


def draw_panel_inverse(key, part):
    first = jax.random.fold_in(key, 0)
    spread = 0.5 / math.sqrt(2.0 * NX)
    noise = jax.random.truncated_normal(first, -4.0, 4.0, (DEPTH_SLABS, 2, NX, NX), jnp.float32)
    scale = 1.0 / math.sqrt(1.25)
    eye = jnp.eye(NX, dtype=jnp.float32)
    real = jnp.clip(scale * (eye + spread * noise[:, 0]), -1.0, 1.0)
    imag = scale * spread * noise[:, 1]
    return jnp.concatenate([real, imag], axis=2).astype(jnp.bfloat16)


def draw_coupling(key, part):
    first, second, final_portion, fourth = jax.random.split(key, 4)
    starting_position = jnp.exp(jax.random.uniform(first, (1, 1, LOAD_VECTORS, LATERAL_POINTS), jnp.float32, math.log(0.25), math.log(0.98)))
    match_tally = jax.random.randint(second, (DEPTH_SLABS, 1, LOAD_VECTORS, LATERAL_POINTS), 0, DEPTH_SLABS) < 2
    contiguous_span = jnp.where(match_tally, jax.random.uniform(final_portion, (DEPTH_SLABS, 1, LOAD_VECTORS, LATERAL_POINTS), jnp.float32, 0.5, 0.8), 1.0)
    phase = jax.random.uniform(fourth, (DEPTH_SLABS, 1, LOAD_VECTORS, LATERAL_POINTS), jnp.float32, -math.pi, math.pi)
    cyclic_period = starting_position * contiguous_span
    return jnp.concatenate([cyclic_period * jnp.cos(phase), cyclic_period * jnp.sin(phase)], axis=1)


def level_of(rng, dims, pieces, least, high):
    loudness = 1.0
    for axis_at, parts in pieces:
        steps = jax.random.uniform(jax.random.fold_in(jax.random.fold_in(rng, 6), axis_at), (parts,), jnp.float32, least / len(pieces), high / len(pieces))
        loudness = loudness * jnp.repeat(jnp.exp(steps), dims[axis_at] // parts).reshape((-1,) + (1,) * (len(dims) - 1 - axis_at))
    return loudness


def scatter_about(own_key, extent, deviation, limit, shards=(), kind=jnp.bfloat16):
    loudness = level_of(own_key, extent, shards, -0.22, 0.18) if shards else 1.0
    values = jax.random.normal(own_key, extent, jnp.float32) * deviation * loudness
    return jnp.minimum(jnp.maximum(values, -limit), limit).astype(kind)


def setup_inputs(seed: int = 0) -> dict:
    seeds = jax.random.split(jax.random.key(seed), 4)
    rhs_field = scatter_about(seeds[0], (DEPTH_SLABS, 2, LOAD_VECTORS, LATERAL_POINTS, NX), 1.0, 6.0, ((0, 32), (4, 8)), jnp.float32)
    panel_inverse = draw_panel_inverse(jax.random.fold_in(seeds[3], 71), 0)
    coupling = draw_coupling(jax.random.fold_in(seeds[3], 71), 0)
    return dict(rhs_field=rhs_field, panel_inverse=panel_inverse, coupling=coupling)


def complex_product(rows, inverse, width):
    flat = rows.reshape(-1, width)
    product = jnp.dot(flat, inverse, preferred_element_type=jnp.float32)
    product = product.reshape(rows.shape[:-1] + (2 * width,))
    real = product[0, ..., :width] - product[1, ..., width:]
    imag = product[0, ..., width:] + product[1, ..., :width]
    return jnp.stack([real, imag])


def twist(factor, field):
    real = factor[0] * field[0] - factor[1] * field[1]
    imag = factor[0] * field[1] + factor[1] * field[0]
    return jnp.stack([real, imag])


def reference(rhs_field, panel_inverse, coupling):
    factors = coupling[..., None]
    start = jnp.zeros(rhs_field.shape[1:], jnp.bfloat16)

    def forward(carried, inputs):
        source, inverse, factor = inputs
        mixed = (source + twist(factor, carried.astype(jnp.float32))).astype(jnp.bfloat16)
        result = complex_product(mixed, inverse, NX)
        return result.astype(jnp.bfloat16), result

    _, forward_all = lax.scan(forward, start, (rhs_field, panel_inverse, factors))

    def backward(carried, inputs):
        starting_position, inverse, factor = inputs
        result = starting_position + complex_product(carried, inverse, NX)
        return twist(factor, result).astype(jnp.bfloat16), result

    _, sweep_field = lax.scan(backward, start, (forward_all, panel_inverse, factors), reverse=True)
    return sweep_field
```

```python
import jax
import jax.numpy as jnp
from jax import lax
from jax.sharding import PartitionSpec as P


def complex_product(rows, inverse, width):
    flat = rows.reshape(-1, width)
    product = jnp.dot(flat, inverse, preferred_element_type=jnp.float32)
    product = product.reshape(rows.shape[:-1] + (2 * width,))
    real = product[0, ..., :width] - product[1, ..., width:]
    imag = product[0, ..., width:] + product[1, ..., :width]
    return jnp.stack([real, imag])


def twist(factor, field):
    real = factor[0] * field[0] - factor[1] * field[1]
    imag = factor[0] * field[1] + factor[1] * field[0]
    return jnp.stack([real, imag])


def body(rhs_field, panel_inverse, coupling):
    lines = lax.all_to_all(rhs_field, "plane", split_axis=3, concat_axis=4, tiled=True)[0]
    inverse = panel_inverse[0]
    factors = coupling[0][..., None]
    width = inverse.shape[0]
    layers = lax.axis_size("layer")
    planes = lax.axis_size("plane")
    place = lax.axis_index("layer")
    plane = lax.axis_index("plane")
    pairs = layers // 2
    down = [(2 * j + 1, 2 * j) for j in range(pairs)]
    ahead = [(2 * j, 2 * j + 2) for j in range(pairs - 1)]
    behind = [(2 * j + 2, 2 * j) for j in range(pairs - 1)]
    back = [(2 * j, 2 * j + 1) for j in range(pairs)]

    rows = width // planes
    piece = lax.dynamic_slice_in_dim(inverse, plane * rows, rows, 0)
    piece = lax.ppermute(piece, "layer", down)
    inverse_next = lax.all_gather(piece, "plane", axis=0, tiled=True)
    lines_next = lax.ppermute(lines, "layer", down)
    factors_next = lax.ppermute(factors, "layer", down)

    def pair_forward(incoming):
        mixed = (lines + twist(factors, incoming.astype(jnp.float32))).astype(jnp.bfloat16)
        first = complex_product(mixed, inverse, width)
        carried = first.astype(jnp.bfloat16).astype(jnp.float32)
        mixed = (lines_next + twist(factors_next, carried)).astype(jnp.bfloat16)
        second = complex_product(mixed, inverse_next, width)
        return first, second

    first, second = pair_forward(jnp.zeros(lines.shape, jnp.bfloat16))
    valid = place == 0
    store_a = jnp.where(valid, first, 0.0)
    store_b = jnp.where(valid, second, 0.0)

    def forward(section, carry):
        store_a, store_b, outgoing = carry
        incoming = lax.ppermute(outgoing, "layer", ahead)
        first, second = pair_forward(incoming)
        valid = place == 2 * section
        store_a = jnp.where(valid, first, store_a)
        store_b = jnp.where(valid, second, store_b)
        return (store_a, store_b, second.astype(jnp.bfloat16))

    store_a, store_b, _ = lax.fori_loop(1, pairs, forward, (store_a, store_b, second.astype(jnp.bfloat16)))

    def pair_backward(sweep_b):
        carried = twist(factors_next, sweep_b).astype(jnp.bfloat16)
        sweep_a = store_a + complex_product(carried, inverse, width)
        return sweep_a, twist(factors, sweep_a).astype(jnp.bfloat16)

    sweep_b = store_b
    sweep_a, outgoing = pair_backward(sweep_b)
    valid = place == layers - 2
    result_a = jnp.where(valid, sweep_a, 0.0)
    result_b = jnp.where(valid, sweep_b, 0.0)

    def backward(section, carry):
        result_a, result_b, outgoing = carry
        incoming = lax.ppermute(outgoing, "layer", behind)
        sweep_b = store_b + complex_product(incoming, inverse_next, width)
        sweep_a, outgoing = pair_backward(sweep_b)
        valid = place == layers - 2 - 2 * section
        result_a = jnp.where(valid, sweep_a, result_a)
        result_b = jnp.where(valid, sweep_b, result_b)
        return (result_a, result_b, outgoing)

    result_a, result_b, _ = lax.fori_loop(1, pairs, backward, (result_a, result_b, outgoing))
    returned = lax.ppermute(result_b, "layer", back)
    result = jnp.where(place % 2 == 0, result_a, returned)
    return lax.all_to_all(result[None], "plane", split_axis=4, concat_axis=3, tiled=True)


def solution(mesh):
    in_specs = (
        P("layer", None, None, None, "plane"),
        P("layer", None, None),
        P("layer", None, None, "plane"),
    )
    out_specs = P("layer", None, None, None, "plane")
    return jax.shard_map(body, mesh=mesh, in_specs=in_specs, out_specs=out_specs, check_vma=False)
```

```python
import jax
import jax.numpy as jnp
from jax import lax
from jax.sharding import PartitionSpec as P


def complex_product(rows, inverse, width):
    flat = rows.reshape(-1, width)
    product = jnp.dot(flat, inverse, preferred_element_type=jnp.float32)
    product = product.reshape(rows.shape[:-1] + (2 * width,))
    real = product[0, ..., :width] - product[1, ..., width:]
    imag = product[0, ..., width:] + product[1, ..., :width]
    return jnp.stack([real, imag])


def twist(factor, field):
    real = factor[0] * field[0] - factor[1] * field[1]
    imag = factor[0] * field[1] + factor[1] * field[0]
    return jnp.stack([real, imag])


def body(rhs_field, panel_inverse, coupling):
    lines = lax.all_to_all(rhs_field, "plane", split_axis=3, concat_axis=4, tiled=True)[0]
    inverse = panel_inverse[0]
    factors = coupling[0][..., None]
    width = inverse.shape[0]
    layers = lax.axis_size("layer")
    planes = lax.axis_size("plane")
    place = lax.axis_index("layer")
    plane = lax.axis_index("plane")
    pairs = layers // 2
    down = [(2 * j + 1, 2 * j) for j in range(pairs)]
    back = [(2 * j, 2 * j + 1) for j in range(pairs)]

    rows = width // planes
    piece = lax.dynamic_slice_in_dim(inverse, plane * rows, rows, 0)
    piece = lax.ppermute(piece, "layer", down)
    inverse_next = lax.all_gather(piece, "plane", axis=0, tiled=True)
    lines_next = lax.ppermute(lines, "layer", down)
    factors_next = lax.ppermute(factors, "layer", down)

    def pair_forward(incoming):
        mixed = (lines + twist(factors, incoming.astype(jnp.float32))).astype(jnp.bfloat16)
        first = complex_product(mixed, inverse, width)
        carried = first.astype(jnp.bfloat16).astype(jnp.float32)
        mixed = (lines_next + twist(factors_next, carried)).astype(jnp.bfloat16)
        second = complex_product(mixed, inverse_next, width)
        return first, second

    zeros = jnp.zeros(lines.shape, jnp.float32)
    outgoing = jnp.zeros(lines.shape, jnp.bfloat16)
    store_a, store_b = zeros, zeros
    for section in range(pairs):
        if section > 0:
            incoming = lax.ppermute(outgoing, "layer", [(2 * section - 2, 2 * section)])
        else:
            incoming = outgoing

        def active(incoming, store_a, store_b, outgoing):
            first, second = pair_forward(incoming)
            return first, second, second.astype(jnp.bfloat16)

        def idle(incoming, store_a, store_b, outgoing):
            return store_a, store_b, outgoing

        store_a, store_b, outgoing = lax.cond(
            place == 2 * section, active, idle, incoming, store_a, store_b, outgoing)

    def pair_backward(sweep_b):
        carried = twist(factors_next, sweep_b).astype(jnp.bfloat16)
        sweep_a = store_a + complex_product(carried, inverse, width)
        return sweep_a, twist(factors, sweep_a).astype(jnp.bfloat16)

    result_a, result_b = zeros, zeros
    for section in range(pairs):
        lead = layers - 2 - 2 * section
        if section > 0:
            incoming = lax.ppermute(outgoing, "layer", [(lead + 2, lead)])
        else:
            incoming = outgoing

        def active(incoming, result_a, result_b, outgoing, first=(section == 0)):
            if first:
                sweep_b = store_b
            else:
                sweep_b = store_b + complex_product(incoming, inverse_next, width)
            sweep_a, outgoing = pair_backward(sweep_b)
            return sweep_a, sweep_b, outgoing

        def idle(incoming, result_a, result_b, outgoing):
            return result_a, result_b, outgoing

        result_a, result_b, outgoing = lax.cond(
            place == lead, active, idle, incoming, result_a, result_b, outgoing)

    returned = lax.ppermute(result_b, "layer", back)
    result = jnp.where(place % 2 == 0, result_a, returned)
    return lax.all_to_all(result[None], "plane", split_axis=4, concat_axis=3, tiled=True)


def solution(mesh):
    in_specs = (
        P("layer", None, None, None, "plane"),
        P("layer", None, None),
        P("layer", None, None, "plane"),
    )
    out_specs = P("layer", None, None, None, "plane")
    return jax.shard_map(body, mesh=mesh, in_specs=in_specs, out_specs=out_specs, check_vma=False)
```

```python
import jax
import jax.numpy as jnp
from jax import lax
from jax.sharding import PartitionSpec as P


def complex_product(real, imag, inverse):
    width = inverse.shape[0]
    rows = jnp.stack([real, imag])
    flat = rows.reshape(-1, width)
    product = jnp.dot(flat, inverse, preferred_element_type=jnp.float32)
    product = product.reshape(rows.shape[:-1] + (2 * width,))
    return (product[0, ..., :width] - product[1, ..., width:],
            product[0, ..., width:] + product[1, ..., :width])


def twist(factor, real, imag):
    return (factor[0] * real - factor[1] * imag, factor[0] * imag + factor[1] * real)


def to_bf16(pair):
    return tuple(part.astype(jnp.bfloat16) for part in pair)


def to_f32(pair):
    return tuple(part.astype(jnp.float32) for part in pair)


def body(rhs_field, panel_inverse, coupling):
    planes = lax.axis_size("plane")
    layers = lax.axis_size("layer")
    place = lax.axis_index("layer")
    plane = lax.axis_index("plane")
    pairs = layers // 2

    block = rhs_field[0]
    parts, loads, ys, chunk = block.shape
    block = block.reshape(parts, loads, planes, ys // planes, chunk)
    block = jnp.moveaxis(block, 2, 0)
    block = lax.all_to_all(block, "plane", split_axis=0, concat_axis=0, tiled=True)
    lines = jnp.moveaxis(block, 0, 3).reshape(parts, loads, ys // planes, planes * chunk)

    inverse = panel_inverse[0]
    factors = coupling[0][..., None]
    width = inverse.shape[0]
    down = [(2 * j + 1, 2 * j) for j in range(pairs)]
    back = [(2 * j, 2 * j + 1) for j in range(pairs)]

    rows = width // planes
    piece = lax.dynamic_slice_in_dim(inverse, plane * rows, rows, 0)
    piece = lax.ppermute(piece, "layer", down)
    inverse_next = lax.all_gather(piece, "plane", axis=0, tiled=True)
    lines_next = lax.ppermute(lines, "layer", down)
    factors_next = lax.ppermute(factors, "layer", down)

    def mix(source, factor, carried):
        twisted = twist(factor, *to_f32(carried))
        return to_bf16((source[0] + twisted[0], source[1] + twisted[1]))

    def pair_forward(incoming):
        first = complex_product(*mix(lines, factors, (incoming[0], incoming[1])), inverse)
        second = complex_product(*mix(lines_next, factors_next, to_bf16(first)), inverse_next)
        return first, second

    zero = jnp.zeros(lines.shape[1:], jnp.float32)
    outgoing = jnp.zeros(lines.shape, jnp.bfloat16)
    store_a, store_b = (zero, zero), (zero, zero)
    for section in range(pairs):
        if section > 0:
            incoming = lax.ppermute(outgoing, "layer", [(2 * section - 2, 2 * section)])
        else:
            incoming = outgoing

        def active(incoming, store_a, store_b, outgoing):
            first, second = pair_forward(incoming)
            return first, second, jnp.stack(to_bf16(second))

        def idle(incoming, store_a, store_b, outgoing):
            return store_a, store_b, outgoing

        store_a, store_b, outgoing = lax.cond(
            place == 2 * section, active, idle, incoming, store_a, store_b, outgoing)

    def pair_backward(sweep_b):
        carried = to_bf16(twist(factors_next, *sweep_b))
        product = complex_product(*carried, inverse)
        sweep_a = (store_a[0] + product[0], store_a[1] + product[1])
        return sweep_a, jnp.stack(to_bf16(twist(factors, *sweep_a)))

    result_a, result_b = (zero, zero), (zero, zero)
    for section in range(pairs):
        lead = layers - 2 - 2 * section
        if section > 0:
            incoming = lax.ppermute(outgoing, "layer", [(lead + 2, lead)])
        else:
            incoming = outgoing

        def active(incoming, result_a, result_b, outgoing, first=(section == 0)):
            if first:
                sweep_b = store_b
            else:
                product = complex_product(incoming[0], incoming[1], inverse_next)
                sweep_b = (store_b[0] + product[0], store_b[1] + product[1])
            sweep_a, outgoing = pair_backward(sweep_b)
            return sweep_a, sweep_b, outgoing

        def idle(incoming, result_a, result_b, outgoing):
            return result_a, result_b, outgoing

        result_a, result_b, outgoing = lax.cond(
            place == lead, active, idle, incoming, result_a, result_b, outgoing)

    returned = lax.ppermute(jnp.stack(result_b), "layer", back)
    result = jnp.where(place % 2 == 0, jnp.stack(result_a), returned)

    result = result.reshape(parts, loads, ys // planes, planes, chunk)
    result = jnp.moveaxis(result, 3, 0)
    result = lax.all_to_all(result, "plane", split_axis=0, concat_axis=0, tiled=True)
    result = jnp.moveaxis(result, 0, 2).reshape(parts, loads, ys, chunk)
    return result[None]


def solution(mesh):
    in_specs = (
        P("layer", None, None, None, "plane"),
        P("layer", None, None),
        P("layer", None, None, "plane"),
    )
    out_specs = P("layer", None, None, None, "plane")
    return jax.shard_map(body, mesh=mesh, in_specs=in_specs, out_specs=out_specs, check_vma=False)
```

```python
import jax
import jax.numpy as jnp
from jax import lax
from jax.experimental import pallas as pl
from jax.experimental.pallas import tpu as pltpu
from jax.sharding import PartitionSpec as P


def kernel_mix(source, factor, carried):
    real = source[0] + (factor[0] * carried[0] - factor[1] * carried[1])
    imag = source[1] + (factor[0] * carried[1] + factor[1] * carried[0])
    return real.astype(jnp.bfloat16), imag.astype(jnp.bfloat16)


def kernel_twist(factor, field):
    real = factor[0] * field[0] - factor[1] * field[1]
    imag = factor[0] * field[1] + factor[1] * field[0]
    return real.astype(jnp.bfloat16), imag.astype(jnp.bfloat16)


def kernel_product(rows, inverse):
    count = rows[0].shape[0]
    width = inverse.shape[0]
    flat = jnp.concatenate(rows, axis=0)
    product = jnp.dot(flat, inverse[...], preferred_element_type=jnp.float32)
    real = product[:count, :width] - product[count:, width:]
    imag = product[:count, width:] + product[count:, :width]
    return real, imag


def read(ref):
    return ref[0], ref[1]


def write(ref, pair):
    ref[0] = pair[0]
    ref[1] = pair[1]


def widen(pair):
    return tuple(part.astype(jnp.bfloat16).astype(jnp.float32) for part in pair)


def forward_kernel(incoming, source, factor, source_next, factor_next, inverse, inverse_next,
                   first_out, second_out, outgoing, held, sems):
    copies = [pltpu.make_async_copy(inverse, held.at[0], sems.at[0]),
              pltpu.make_async_copy(inverse_next, held.at[1], sems.at[1])]
    for copy in copies:
        copy.start()
    carried = tuple(part.astype(jnp.float32) for part in read(incoming))
    mixed = kernel_mix(read(source), read(factor), carried)
    copies[0].wait()
    first = kernel_product(mixed, held.at[0])
    write(first_out, first)
    mixed = kernel_mix(read(source_next), read(factor_next), widen(first))
    copies[1].wait()
    second = kernel_product(mixed, held.at[1])
    write(second_out, second)
    write(outgoing, tuple(part.astype(jnp.bfloat16) for part in second))


def backward_kernel(skip, incoming, store_a, store_b, factor, factor_next, inverse, inverse_next,
                    sweep_a_out, sweep_b_out, outgoing, held, sems):
    copies = [pltpu.make_async_copy(inverse, held.at[0], sems.at[0])]
    if not skip:
        copies.append(pltpu.make_async_copy(inverse_next, held.at[1], sems.at[1]))
    for copy in copies:
        copy.start()
    sweep_b = read(store_b)
    if not skip:
        copies[1].wait()
        product = kernel_product(read(incoming), held.at[1])
        sweep_b = (sweep_b[0] + product[0], sweep_b[1] + product[1])
    write(sweep_b_out, sweep_b)
    carried = kernel_twist(read(factor_next), sweep_b)
    copies[0].wait()
    product = kernel_product(carried, held.at[0])
    store = read(store_a)
    sweep_a = (store[0] + product[0], store[1] + product[1])
    write(sweep_a_out, sweep_a)
    write(outgoing, kernel_twist(read(factor), sweep_a))


def pair_call(kernel, args, shape, width, matmuls):
    local = pl.BlockSpec(memory_space=pltpu.VMEM)
    remote = pl.BlockSpec(memory_space=pl.ANY)
    rows = 2 * shape[0] * shape[1]
    return pl.pallas_call(
        kernel,
        out_shape=(jax.ShapeDtypeStruct(shape, jnp.float32),
                   jax.ShapeDtypeStruct(shape, jnp.float32),
                   jax.ShapeDtypeStruct(shape, jnp.bfloat16)),
        in_specs=[local] * (len(args) - 2) + [remote, remote],
        out_specs=(local, local, local),
        scratch_shapes=[pltpu.VMEM((2, width, 2 * width), jnp.bfloat16),
                        pltpu.SemaphoreType.DMA((2,))],
        compiler_params=pltpu.CompilerParams(vmem_limit_bytes=48 * 1024 * 1024),
        cost_estimate=pl.CostEstimate(
            flops=matmuls * 2 * rows * width * 2 * width, transcendentals=0,
            bytes_accessed=matmuls * width * 2 * width * 2 + 8 * rows * width * 4),
    )(*args)


def body(rhs_field, panel_inverse, coupling):
    planes = lax.axis_size("plane")
    layers = lax.axis_size("layer")
    place = lax.axis_index("layer")
    plane = lax.axis_index("plane")
    pairs = layers // 2

    block = rhs_field[0]
    parts, loads, ys, chunk = block.shape
    block = block.reshape(parts, loads, planes, ys // planes, chunk)
    block = jnp.moveaxis(block, 2, 0)
    block = lax.all_to_all(block, "plane", split_axis=0, concat_axis=0, tiled=True)
    lines = jnp.moveaxis(block, 0, 3).reshape(parts, loads * ys // planes, planes * chunk)
    shape = lines.shape

    inverse = panel_inverse[0]
    width = inverse.shape[0]
    factors = jnp.broadcast_to(coupling[0].reshape(parts, shape[1], 1), shape)
    down = [(2 * j + 1, 2 * j) for j in range(pairs)]
    back = [(2 * j, 2 * j + 1) for j in range(pairs)]

    rows = width // planes
    piece = lax.dynamic_slice_in_dim(inverse, plane * rows, rows, 0)
    piece = lax.ppermute(piece, "layer", down)
    inverse_next = lax.all_gather(piece, "plane", axis=0, tiled=True)
    lines_next = lax.ppermute(lines, "layer", down)
    factors_next = lax.ppermute(factors, "layer", down)

    zero = jnp.zeros(shape, jnp.float32)
    outgoing = jnp.zeros(shape, jnp.bfloat16)
    store_a, store_b = zero, zero
    for section in range(pairs):
        if section > 0:
            incoming = lax.ppermute(outgoing, "layer", [(2 * section - 2, 2 * section)])
        else:
            incoming = outgoing

        def active(incoming, store_a, store_b, outgoing):
            args = (incoming, lines, factors, lines_next, factors_next, inverse, inverse_next)
            return pair_call(forward_kernel, args, shape, width, 2)

        def idle(incoming, store_a, store_b, outgoing):
            return store_a, store_b, outgoing

        store_a, store_b, outgoing = lax.cond(
            place == 2 * section, active, idle, incoming, store_a, store_b, outgoing)

    result_a, result_b = zero, zero
    for section in range(pairs):
        lead = layers - 2 - 2 * section
        if section > 0:
            incoming = lax.ppermute(outgoing, "layer", [(lead + 2, lead)])
        else:
            incoming = outgoing

        def active(incoming, result_a, result_b, outgoing, skip=(section == 0)):
            kernel = lambda *refs: backward_kernel(skip, *refs)
            args = (incoming, store_a, store_b, factors, factors_next, inverse, inverse_next)
            return pair_call(kernel, args, shape, width, 1 if skip else 2)

        def idle(incoming, result_a, result_b, outgoing):
            return result_a, result_b, outgoing

        result_a, result_b, outgoing = lax.cond(
            place == lead, active, idle, incoming, result_a, result_b, outgoing)

    returned = lax.ppermute(result_b, "layer", back)
    result = jnp.where(place % 2 == 0, result_a, returned)

    result = result.reshape(parts, loads, ys // planes, planes, chunk)
    result = jnp.moveaxis(result, 3, 0)
    result = lax.all_to_all(result, "plane", split_axis=0, concat_axis=0, tiled=True)
    result = jnp.moveaxis(result, 0, 2).reshape(parts, loads, ys, chunk)
    return result[None]


def solution(mesh):
    in_specs = (
        P("layer", None, None, None, "plane"),
        P("layer", None, None),
        P("layer", None, None, "plane"),
    )
    out_specs = P("layer", None, None, None, "plane")
    return jax.shard_map(body, mesh=mesh, in_specs=in_specs, out_specs=out_specs, check_vma=False)
```

```python
import jax
import jax.numpy as jnp
from jax import lax
from jax.experimental import pallas as pl
from jax.experimental.pallas import tpu as pltpu
from jax.sharding import PartitionSpec as P


def kernel_mix(source, factor, carried):
    real = source[0] + (factor[0] * carried[0] - factor[1] * carried[1])
    imag = source[1] + (factor[0] * carried[1] + factor[1] * carried[0])
    return real.astype(jnp.bfloat16), imag.astype(jnp.bfloat16)


def kernel_twist(factor, field):
    real = factor[0] * field[0] - factor[1] * field[1]
    imag = factor[0] * field[1] + factor[1] * field[0]
    return real.astype(jnp.bfloat16), imag.astype(jnp.bfloat16)


def kernel_product(rows, inverse):
    count = rows[0].shape[0]
    width = inverse.shape[0]
    flat = jnp.concatenate(rows, axis=0)
    product = jnp.dot(flat, inverse[...], preferred_element_type=jnp.float32)
    real = product[:count, :width] - product[count:, width:]
    imag = product[:count, width:] + product[count:, :width]
    return real, imag


def read(ref):
    return ref[0], ref[1]


def write(ref, pair):
    ref[0] = pair[0]
    ref[1] = pair[1]


def widen(pair):
    return tuple(part.astype(jnp.bfloat16).astype(jnp.float32) for part in pair)


def forward_kernel(single, *refs):
    if single:
        incoming, source, factor, inverse, first_out, outgoing, held, sems = refs
    else:
        (incoming, source, factor, source_next, factor_next, inverse, inverse_next,
         first_out, second_out, outgoing, held, sems) = refs
    copy = pltpu.make_async_copy(inverse, held.at[0], sems.at[0])
    copy.start()
    carried = tuple(part.astype(jnp.float32) for part in read(incoming))
    mixed = kernel_mix(read(source), read(factor), carried)
    copy.wait()
    if not single:
        copy = pltpu.make_async_copy(inverse_next, held.at[1], sems.at[1])
        copy.start()
    first = kernel_product(mixed, held.at[0])
    write(first_out, first)
    if single:
        write(outgoing, tuple(part.astype(jnp.bfloat16) for part in first))
        return
    mixed = kernel_mix(read(source_next), read(factor_next), widen(first))
    copy.wait()
    second = kernel_product(mixed, held.at[1])
    write(second_out, second)
    write(outgoing, tuple(part.astype(jnp.bfloat16) for part in second))


def backward_kernel(skip, incoming, store_a, store_b, factor, factor_next, inverse, inverse_next,
                    sweep_a_out, sweep_b_out, outgoing, held, sems):
    sweep_b = read(store_b)
    if not skip:
        copy = pltpu.make_async_copy(inverse_next, held.at[1], sems.at[1])
        copy.start()
        copy.wait()
    copy_own = pltpu.make_async_copy(inverse, held.at[0], sems.at[0])
    copy_own.start()
    if not skip:
        product = kernel_product(read(incoming), held.at[1])
        sweep_b = (sweep_b[0] + product[0], sweep_b[1] + product[1])
    write(sweep_b_out, sweep_b)
    carried = kernel_twist(read(factor_next), sweep_b)
    copy_own.wait()
    product = kernel_product(carried, held.at[0])
    store = read(store_a)
    sweep_a = (store[0] + product[0], store[1] + product[1])
    write(sweep_a_out, sweep_a)
    write(outgoing, kernel_twist(read(factor), sweep_a))


def pair_call(kernel, args, shape, width, matmuls, remotes, results):
    local = pl.BlockSpec(memory_space=pltpu.VMEM)
    remote = pl.BlockSpec(memory_space=pl.ANY)
    rows = 2 * shape[0] * shape[1]
    out_shape = [jax.ShapeDtypeStruct(shape, jnp.float32)] * (results - 1)
    out_shape.append(jax.ShapeDtypeStruct(shape, jnp.bfloat16))
    return pl.pallas_call(
        kernel,
        out_shape=tuple(out_shape),
        in_specs=[local] * (len(args) - remotes) + [remote] * remotes,
        out_specs=tuple([local] * results),
        scratch_shapes=[pltpu.VMEM((2, width, 2 * width), jnp.bfloat16),
                        pltpu.SemaphoreType.DMA((2,))],
        compiler_params=pltpu.CompilerParams(vmem_limit_bytes=48 * 1024 * 1024),
        cost_estimate=pl.CostEstimate(
            flops=matmuls * 2 * rows * width * 2 * width, transcendentals=0,
            bytes_accessed=matmuls * width * 2 * width * 2 + 8 * rows * width * 4),
    )(*args)


def body(rhs_field, panel_inverse, coupling):
    planes = lax.axis_size("plane")
    layers = lax.axis_size("layer")
    place = lax.axis_index("layer")
    plane = lax.axis_index("plane")
    pairs = layers // 2

    block = rhs_field[0]
    parts, loads, ys, chunk = block.shape
    block = block.reshape(parts, loads, planes, ys // planes, chunk)
    block = jnp.moveaxis(block, 2, 0)
    block = lax.all_to_all(block, "plane", split_axis=0, concat_axis=0, tiled=True)
    lines = jnp.moveaxis(block, 0, 3).reshape(parts, loads * ys // planes, planes * chunk)
    shape = lines.shape

    inverse = panel_inverse[0]
    width = inverse.shape[0]
    factors = jnp.broadcast_to(coupling[0].reshape(parts, shape[1], 1), shape)
    down = [(2 * j + 1, 2 * j) for j in range(pairs)]
    back = [(2 * j, 2 * j + 1) for j in range(pairs)]

    rows = width // planes
    piece = lax.dynamic_slice_in_dim(inverse, plane * rows, rows, 0)
    piece = lax.ppermute(piece, "layer", down)
    inverse_next = lax.all_gather(piece, "plane", axis=0, tiled=True)
    lines_next = lax.ppermute(lines, "layer", down)
    factors_next = lax.ppermute(factors, "layer", down)

    zero = jnp.zeros(shape, jnp.float32)
    outgoing = jnp.zeros(shape, jnp.bfloat16)
    store_a, store_b = zero, zero
    for panel in range(2):
        if panel > 0:
            incoming = lax.ppermute(outgoing, "layer", [(panel - 1, panel)])
        else:
            incoming = outgoing

        def active(incoming, store_a, outgoing):
            kernel = lambda *refs: forward_kernel(True, *refs)
            return pair_call(kernel, (incoming, lines, factors, inverse), shape, width, 1, 1, 2)

        def idle(incoming, store_a, outgoing):
            return store_a, outgoing

        store_a, outgoing = lax.cond(place == panel, active, idle, incoming, store_a, outgoing)
    store_b = lax.ppermute(store_a, "layer", [(1, 0)])

    for section in range(1, pairs):
        source = 1 if section == 1 else 2 * section - 2
        incoming = lax.ppermute(outgoing, "layer", [(source, 2 * section)])

        def active(incoming, store_a, store_b, outgoing):
            kernel = lambda *refs: forward_kernel(False, *refs)
            args = (incoming, lines, factors, lines_next, factors_next, inverse, inverse_next)
            return pair_call(kernel, args, shape, width, 2, 2, 3)

        def idle(incoming, store_a, store_b, outgoing):
            return store_a, store_b, outgoing

        store_a, store_b, outgoing = lax.cond(
            place == 2 * section, active, idle, incoming, store_a, store_b, outgoing)

    result_a, result_b = zero, zero
    for section in range(pairs):
        lead = layers - 2 - 2 * section
        if section > 0:
            incoming = lax.ppermute(outgoing, "layer", [(lead + 2, lead)])
        else:
            incoming = outgoing

        def active(incoming, result_a, result_b, outgoing, skip=(section == 0)):
            kernel = lambda *refs: backward_kernel(skip, *refs)
            args = (incoming, store_a, store_b, factors, factors_next, inverse, inverse_next)
            return pair_call(kernel, args, shape, width, 1 if skip else 2, 2, 3)

        def idle(incoming, result_a, result_b, outgoing):
            return result_a, result_b, outgoing

        result_a, result_b, outgoing = lax.cond(
            place == lead, active, idle, incoming, result_a, result_b, outgoing)

    returned = lax.ppermute(result_b, "layer", back)
    result = jnp.where(place % 2 == 0, result_a, returned)

    result = result.reshape(parts, loads, ys // planes, planes, chunk)
    result = jnp.moveaxis(result, 3, 0)
    result = lax.all_to_all(result, "plane", split_axis=0, concat_axis=0, tiled=True)
    result = jnp.moveaxis(result, 0, 2).reshape(parts, loads, ys, chunk)
    return result[None]


def solution(mesh):
    in_specs = (
        P("layer", None, None, None, "plane"),
        P("layer", None, None),
        P("layer", None, None, "plane"),
    )
    out_specs = P("layer", None, None, None, "plane")
    return jax.shard_map(body, mesh=mesh, in_specs=in_specs, out_specs=out_specs, check_vma=False)
```

```python
import jax
import jax.numpy as jnp
from jax import lax
from jax.experimental import pallas as pl
from jax.experimental.pallas import tpu as pltpu
from jax.sharding import PartitionSpec as P


def kernel_mix(source, factor, carried):
    real = source[0] + (factor[0] * carried[0] - factor[1] * carried[1])
    imag = source[1] + (factor[0] * carried[1] + factor[1] * carried[0])
    return real.astype(jnp.bfloat16), imag.astype(jnp.bfloat16)


def kernel_twist(factor, field):
    real = factor[0] * field[0] - factor[1] * field[1]
    imag = factor[0] * field[1] + factor[1] * field[0]
    return real.astype(jnp.bfloat16), imag.astype(jnp.bfloat16)


def kernel_product(rows, inverse):
    count = rows[0].shape[0]
    width = inverse.shape[0]
    flat = jnp.concatenate(rows, axis=0)
    product = jnp.dot(flat, inverse[...], preferred_element_type=jnp.float32)
    real = product[:count, :width] - product[count:, width:]
    imag = product[:count, width:] + product[count:, :width]
    return real, imag


def read(ref):
    return ref[0], ref[1]


def write(ref, pair):
    ref[0] = pair[0]
    ref[1] = pair[1]


def widen(pair):
    return tuple(part.astype(jnp.bfloat16).astype(jnp.float32) for part in pair)


def forward_kernel(single, *refs):
    if single:
        incoming, source, factor, inverse, first_out, outgoing, held, sems = refs
    else:
        (incoming, source, factor, source_next, factor_next, inverse, inverse_next,
         first_out, second_out, outgoing, held, sems) = refs
    copies = [pltpu.make_async_copy(inverse, held.at[0], sems.at[0])]
    if not single:
        copies.append(pltpu.make_async_copy(inverse_next, held.at[1], sems.at[1]))
    for copy in copies:
        copy.start()
    carried = tuple(part.astype(jnp.float32) for part in read(incoming))
    mixed = kernel_mix(read(source), read(factor), carried)
    copies[0].wait()
    first = kernel_product(mixed, held.at[0])
    write(first_out, first)
    if single:
        write(outgoing, tuple(part.astype(jnp.bfloat16) for part in first))
        return
    mixed = kernel_mix(read(source_next), read(factor_next), widen(first))
    copies[1].wait()
    second = kernel_product(mixed, held.at[1])
    write(second_out, second)
    write(outgoing, tuple(part.astype(jnp.bfloat16) for part in second))


def quad_kernel(skip, incoming, *refs):
    stores, factors, inverses = refs[0:4], refs[4:8], refs[8:12]
    sweeps, outgoing, held, sems = refs[12:16], refs[16], refs[17], refs[18]
    order = [2, 1, 0] if skip else [3, 2, 1, 0]
    copies = {i: pltpu.make_async_copy(inverses[i], held.at[i], sems.at[i]) for i in order}
    for panel in order[:2]:
        copies[panel].start()
    queued = 2
    carried = read(incoming)
    for panel in (3, 2, 1, 0):
        store = read(stores[panel])
        if skip and panel == 3:
            sweep = store
        else:
            copies[panel].wait()
            if queued < len(order):
                copies[order[queued]].start()
                queued += 1
            product = kernel_product(carried, held.at[panel])
            sweep = (store[0] + product[0], store[1] + product[1])
        write(sweeps[panel], sweep)
        carried = kernel_twist(read(factors[panel]), sweep)
    write(outgoing, carried)


def quad_call(skip, args, shape, width):
    local = pl.BlockSpec(memory_space=pltpu.VMEM)
    remote = pl.BlockSpec(memory_space=pl.ANY)
    rows = 2 * shape[0] * shape[1]
    matmuls = 3 if skip else 4
    out_shape = [jax.ShapeDtypeStruct(shape, jnp.float32)] * 4
    out_shape.append(jax.ShapeDtypeStruct(shape, jnp.bfloat16))
    return pl.pallas_call(
        lambda *refs: quad_kernel(skip, *refs),
        out_shape=tuple(out_shape),
        in_specs=[local] * 9 + [remote] * 4,
        out_specs=tuple([local] * 5),
        scratch_shapes=[pltpu.VMEM((4, width, 2 * width), jnp.bfloat16),
                        pltpu.SemaphoreType.DMA((4,))],
        compiler_params=pltpu.CompilerParams(vmem_limit_bytes=56 * 1024 * 1024),
        cost_estimate=pl.CostEstimate(
            flops=matmuls * 2 * rows * width * 2 * width, transcendentals=0,
            bytes_accessed=matmuls * width * 2 * width * 2 + 14 * rows * width * 4),
    )(*args)


def pair_call(kernel, args, shape, width, matmuls, remotes, results):
    local = pl.BlockSpec(memory_space=pltpu.VMEM)
    remote = pl.BlockSpec(memory_space=pl.ANY)
    rows = 2 * shape[0] * shape[1]
    out_shape = [jax.ShapeDtypeStruct(shape, jnp.float32)] * (results - 1)
    out_shape.append(jax.ShapeDtypeStruct(shape, jnp.bfloat16))
    return pl.pallas_call(
        kernel,
        out_shape=tuple(out_shape),
        in_specs=[local] * (len(args) - remotes) + [remote] * remotes,
        out_specs=tuple([local] * results),
        scratch_shapes=[pltpu.VMEM((2, width, 2 * width), jnp.bfloat16),
                        pltpu.SemaphoreType.DMA((2,))],
        compiler_params=pltpu.CompilerParams(vmem_limit_bytes=48 * 1024 * 1024),
        cost_estimate=pl.CostEstimate(
            flops=matmuls * 2 * rows * width * 2 * width, transcendentals=0,
            bytes_accessed=matmuls * width * 2 * width * 2 + 8 * rows * width * 4),
    )(*args)


def body(rhs_field, panel_inverse, coupling):
    planes = lax.axis_size("plane")
    layers = lax.axis_size("layer")
    place = lax.axis_index("layer")
    plane = lax.axis_index("plane")
    pairs = layers // 2

    block = rhs_field[0]
    parts, loads, ys, chunk = block.shape
    block = block.reshape(parts, loads, planes, ys // planes, chunk)
    block = jnp.moveaxis(block, 2, 0)
    block = lax.all_to_all(block, "plane", split_axis=0, concat_axis=0, tiled=True)
    lines = jnp.moveaxis(block, 0, 3).reshape(parts, loads * ys // planes, planes * chunk)
    shape = lines.shape

    inverse = panel_inverse[0]
    width = inverse.shape[0]
    factors = jnp.broadcast_to(coupling[0].reshape(parts, shape[1], 1), shape)
    down = [(2 * j + 1, 2 * j) for j in range(pairs)]

    rows = width // planes
    piece = lax.dynamic_slice_in_dim(inverse, plane * rows, rows, 0)
    own_piece = piece
    piece = lax.ppermute(piece, "layer", down)
    inverse_next = lax.all_gather(piece, "plane", axis=0, tiled=True)
    quads = layers // 4
    _, own_piece = lax.optimization_barrier((inverse_next, own_piece))
    quad_inverses = [
        lax.all_gather(lax.ppermute(own_piece, "layer", [(4 * j + offset, 4 * j) for j in range(quads)]),
                       "plane", axis=0, tiled=True)
        for offset in (2, 3)]
    lines_next = lax.ppermute(lines, "layer", down)
    factors_next = lax.ppermute(factors, "layer", down)

    zero = jnp.zeros(shape, jnp.float32)
    outgoing = jnp.zeros(shape, jnp.bfloat16)
    store_a, store_b = zero, zero
    for panel in range(2):
        if panel > 0:
            incoming = lax.ppermute(outgoing, "layer", [(panel - 1, panel)])
        else:
            incoming = outgoing

        def active(incoming, store_a, outgoing):
            kernel = lambda *refs: forward_kernel(True, *refs)
            return pair_call(kernel, (incoming, lines, factors, inverse), shape, width, 1, 1, 2)

        def idle(incoming, store_a, outgoing):
            return store_a, outgoing

        store_a, outgoing = lax.cond(place == panel, active, idle, incoming, store_a, outgoing)
    store_b = lax.ppermute(store_a, "layer", [(1, 0)])

    for section in range(1, pairs):
        source = 1 if section == 1 else 2 * section - 2
        incoming = lax.ppermute(outgoing, "layer", [(source, 2 * section)])

        def active(incoming, store_a, store_b, outgoing):
            kernel = lambda *refs: forward_kernel(False, *refs)
            args = (incoming, lines, factors, lines_next, factors_next, inverse, inverse_next)
            return pair_call(kernel, args, shape, width, 2, 2, 3)

        def idle(incoming, store_a, store_b, outgoing):
            return store_a, store_b, outgoing

        store_a, store_b, outgoing = lax.cond(
            place == 2 * section, active, idle, incoming, store_a, store_b, outgoing)

    gather = [(4 * j + 2, 4 * j) for j in range(quads)]
    quad_stores = [lax.ppermute(store, "layer", gather) for store in (store_a, store_b)]
    quad_factors = [lax.ppermute(factor, "layer", gather) for factor in (factors, factors_next)]

    sweeps = (zero, zero, zero, zero)
    for section in range(quads):
        lead = layers - 4 - 4 * section
        if section > 0:
            incoming = lax.ppermute(outgoing, "layer", [(lead + 4, lead)])
        else:
            incoming = outgoing

        def active(incoming, sweeps, outgoing, skip=(section == 0)):
            args = ((incoming, store_a, store_b) + tuple(quad_stores) + (factors, factors_next)
                    + tuple(quad_factors) + (inverse, inverse_next) + tuple(quad_inverses))
            results = quad_call(skip, args, shape, width)
            return tuple(results[:4]), results[4]

        def idle(incoming, sweeps, outgoing):
            return sweeps, outgoing

        sweeps, outgoing = lax.cond(place == lead, active, idle, incoming, sweeps, outgoing)

    result = sweeps[0]
    for offset in (1, 2, 3):
        returned = lax.ppermute(sweeps[offset], "layer", [(4 * j, 4 * j + offset) for j in range(quads)])
        result = jnp.where(place % 4 == offset, returned, result)

    result = result.reshape(parts, loads, ys // planes, planes, chunk)
    result = jnp.moveaxis(result, 3, 0)
    result = lax.all_to_all(result, "plane", split_axis=0, concat_axis=0, tiled=True)
    result = jnp.moveaxis(result, 0, 2).reshape(parts, loads, ys, chunk)
    return result[None]


def solution(mesh):
    in_specs = (
        P("layer", None, None, None, "plane"),
        P("layer", None, None),
        P("layer", None, None, "plane"),
    )
    out_specs = P("layer", None, None, None, "plane")
    return jax.shard_map(body, mesh=mesh, in_specs=in_specs, out_specs=out_specs, check_vma=False)
```

```python
import jax
import jax.numpy as jnp
from jax import lax
from jax.experimental import pallas as pl
from jax.experimental.pallas import tpu as pltpu
from jax.sharding import PartitionSpec as P


def kernel_mix(source, factor, carried):
    real = source[0] + (factor[0] * carried[0] - factor[1] * carried[1])
    imag = source[1] + (factor[0] * carried[1] + factor[1] * carried[0])
    return real.astype(jnp.bfloat16), imag.astype(jnp.bfloat16)


def kernel_twist(factor, field):
    real = factor[0] * field[0] - factor[1] * field[1]
    imag = factor[0] * field[1] + factor[1] * field[0]
    return real.astype(jnp.bfloat16), imag.astype(jnp.bfloat16)


def kernel_product(rows, inverse):
    count = rows[0].shape[0]
    width = inverse.shape[0]
    flat = jnp.concatenate(rows, axis=0)
    product = jnp.dot(flat, inverse[...], preferred_element_type=jnp.float32)
    real = product[:count, :width] - product[count:, width:]
    imag = product[:count, width:] + product[count:, :width]
    return real, imag


def read(ref):
    return ref[0], ref[1]


def write(ref, pair):
    ref[0] = pair[0]
    ref[1] = pair[1]


def widen(pair):
    return tuple(part.astype(jnp.bfloat16).astype(jnp.float32) for part in pair)


def forward_kernel(single, *refs):
    if single:
        incoming, source, factor, inverse, first_out, outgoing, held, sems = refs
    else:
        (incoming, source, factor, source_next, factor_next, inverse, inverse_next,
         first_out, second_out, outgoing, held, sems) = refs
    copies = [pltpu.make_async_copy(inverse, held.at[0], sems.at[0])]
    if not single:
        copies.append(pltpu.make_async_copy(inverse_next, held.at[1], sems.at[1]))
    for copy in copies:
        copy.start()
    carried = tuple(part.astype(jnp.float32) for part in read(incoming))
    mixed = kernel_mix(read(source), read(factor), carried)
    copies[0].wait()
    first = kernel_product(mixed, held.at[0])
    write(first_out, first)
    if single:
        write(outgoing, tuple(part.astype(jnp.bfloat16) for part in first))
        return
    mixed = kernel_mix(read(source_next), read(factor_next), widen(first))
    copies[1].wait()
    second = kernel_product(mixed, held.at[1])
    write(second_out, second)
    write(outgoing, tuple(part.astype(jnp.bfloat16) for part in second))


def quad_kernel(skip, incoming, *refs):
    stores, factors, inverses = refs[0:4], refs[4:8], refs[8:12]
    sweeps, outgoing, held, sems = refs[12:16], refs[16], refs[17], refs[18]
    order = [2, 1, 0] if skip else [3, 2, 1, 0]
    copies = {i: pltpu.make_async_copy(inverses[i], held.at[i], sems.at[i]) for i in order}
    for panel in order[:2]:
        copies[panel].start()
    queued = 2
    carried = read(incoming)
    for panel in (3, 2, 1, 0):
        store = read(stores[panel])
        if skip and panel == 3:
            sweep = store
        else:
            copies[panel].wait()
            if queued < len(order):
                copies[order[queued]].start()
                queued += 1
            product = kernel_product(carried, held.at[panel])
            sweep = (store[0] + product[0], store[1] + product[1])
        write(sweeps[panel], sweep)
        carried = kernel_twist(read(factors[panel]), sweep)
    write(outgoing, carried)


def quad_call(skip, args, shape, width):
    local = pl.BlockSpec(memory_space=pltpu.VMEM)
    remote = pl.BlockSpec(memory_space=pl.ANY)
    rows = 2 * shape[0] * shape[1]
    matmuls = 3 if skip else 4
    out_shape = [jax.ShapeDtypeStruct(shape, jnp.float32)] * 4
    out_shape.append(jax.ShapeDtypeStruct(shape, jnp.bfloat16))
    return pl.pallas_call(
        lambda *refs: quad_kernel(skip, *refs),
        out_shape=tuple(out_shape),
        in_specs=[local] * 9 + [remote] * 4,
        out_specs=tuple([local] * 5),
        scratch_shapes=[pltpu.VMEM((4, width, 2 * width), jnp.bfloat16),
                        pltpu.SemaphoreType.DMA((4,))],
        compiler_params=pltpu.CompilerParams(vmem_limit_bytes=56 * 1024 * 1024),
        cost_estimate=pl.CostEstimate(
            flops=matmuls * 2 * rows * width * 2 * width, transcendentals=0,
            bytes_accessed=matmuls * width * 2 * width * 2 + 14 * rows * width * 4),
    )(*args)


def pair_call(kernel, args, shape, width, matmuls, remotes, results):
    local = pl.BlockSpec(memory_space=pltpu.VMEM)
    remote = pl.BlockSpec(memory_space=pl.ANY)
    rows = 2 * shape[0] * shape[1]
    out_shape = [jax.ShapeDtypeStruct(shape, jnp.float32)] * (results - 1)
    out_shape.append(jax.ShapeDtypeStruct(shape, jnp.bfloat16))
    return pl.pallas_call(
        kernel,
        out_shape=tuple(out_shape),
        in_specs=[local] * (len(args) - remotes) + [remote] * remotes,
        out_specs=tuple([local] * results),
        scratch_shapes=[pltpu.VMEM((2, width, 2 * width), jnp.bfloat16),
                        pltpu.SemaphoreType.DMA((2,))],
        compiler_params=pltpu.CompilerParams(vmem_limit_bytes=48 * 1024 * 1024),
        cost_estimate=pl.CostEstimate(
            flops=matmuls * 2 * rows * width * 2 * width, transcendentals=0,
            bytes_accessed=matmuls * width * 2 * width * 2 + 8 * rows * width * 4),
    )(*args)


def body(rhs_field, panel_inverse, coupling):
    planes = lax.axis_size("plane")
    layers = lax.axis_size("layer")
    place = lax.axis_index("layer")
    plane = lax.axis_index("plane")
    pairs = layers // 2

    block = rhs_field[0]
    parts, loads, ys, chunk = block.shape
    block = block.reshape(parts, loads, planes, ys // planes, chunk)
    block = jnp.moveaxis(block, 2, 0)
    block = lax.all_to_all(block, "plane", split_axis=0, concat_axis=0, tiled=True)
    lines = jnp.moveaxis(block, 0, 3).reshape(parts, loads * ys // planes, planes * chunk)
    shape = lines.shape

    inverse = panel_inverse[0]
    width = inverse.shape[0]
    factors = jnp.broadcast_to(coupling[0].reshape(parts, shape[1], 1), shape)
    down = [(2 * j + 1, 2 * j) for j in range(pairs)]

    rows = width // planes
    piece = lax.dynamic_slice_in_dim(inverse, plane * rows, rows, 0)
    own_piece = piece
    piece = lax.ppermute(piece, "layer", down)
    inverse_next = lax.all_gather(piece, "plane", axis=0, tiled=True)
    lines_next = lax.ppermute(lines, "layer", down)
    factors_next = lax.ppermute(factors, "layer", down)
    quads = layers // 4
    gather = [(4 * j + 2, 4 * j) for j in range(quads)]
    quad_factors = [lax.ppermute(factor, "layer", gather) for factor in (factors, factors_next)]

    zero = jnp.zeros(shape, jnp.float32)
    outgoing = jnp.zeros(shape, jnp.bfloat16)
    store_a, store_b = zero, zero
    for panel in range(2):
        if panel > 0:
            incoming = lax.ppermute(outgoing, "layer", [(panel - 1, panel)])
        else:
            incoming = outgoing

        def active(incoming, store_a, outgoing):
            kernel = lambda *refs: forward_kernel(True, *refs)
            return pair_call(kernel, (incoming, lines, factors, inverse), shape, width, 1, 1, 2)

        def idle(incoming, store_a, outgoing):
            return store_a, outgoing

        store_a, outgoing = lax.cond(place == panel, active, idle, incoming, store_a, outgoing)
    store_b = lax.ppermute(store_a, "layer", [(1, 0)])

    for section in range(1, pairs):
        source = 1 if section == 1 else 2 * section - 2
        incoming = lax.ppermute(outgoing, "layer", [(source, 2 * section)])

        def active(incoming, store_a, store_b, outgoing):
            kernel = lambda *refs: forward_kernel(False, *refs)
            args = (incoming, lines, factors, lines_next, factors_next, inverse, inverse_next)
            return pair_call(kernel, args, shape, width, 2, 2, 3)

        def idle(incoming, store_a, store_b, outgoing):
            return store_a, store_b, outgoing

        store_a, store_b, outgoing = lax.cond(
            place == 2 * section, active, idle, incoming, store_a, store_b, outgoing)
        if section == min(7, pairs - 1):
            outgoing, moved = lax.optimization_barrier((outgoing, own_piece))
            quad_inverses = [
                lax.all_gather(lax.ppermute(moved, "layer", [(4 * j + offset, 4 * j) for j in range(quads)]),
                               "plane", axis=0, tiled=True)
                for offset in (2, 3)]

    quad_stores = [lax.ppermute(store, "layer", gather) for store in (store_a, store_b)]

    sweeps = (zero, zero, zero, zero)
    for section in range(quads):
        lead = layers - 4 - 4 * section
        if section > 0:
            incoming = lax.ppermute(outgoing, "layer", [(lead + 4, lead)])
        else:
            incoming = outgoing

        def active(incoming, sweeps, outgoing, skip=(section == 0)):
            args = ((incoming, store_a, store_b) + tuple(quad_stores) + (factors, factors_next)
                    + tuple(quad_factors) + (inverse, inverse_next) + tuple(quad_inverses))
            results = quad_call(skip, args, shape, width)
            return tuple(results[:4]), results[4]

        def idle(incoming, sweeps, outgoing):
            return sweeps, outgoing

        sweeps, outgoing = lax.cond(place == lead, active, idle, incoming, sweeps, outgoing)

    result = sweeps[0]
    for offset in (1, 2, 3):
        returned = lax.ppermute(sweeps[offset], "layer", [(4 * j, 4 * j + offset) for j in range(quads)])
        result = jnp.where(place % 4 == offset, returned, result)

    result = result.reshape(parts, loads, ys // planes, planes, chunk)
    result = jnp.moveaxis(result, 3, 0)
    result = lax.all_to_all(result, "plane", split_axis=0, concat_axis=0, tiled=True)
    result = jnp.moveaxis(result, 0, 2).reshape(parts, loads, ys, chunk)
    return result[None]


def solution(mesh):
    in_specs = (
        P("layer", None, None, None, "plane"),
        P("layer", None, None),
        P("layer", None, None, "plane"),
    )
    out_specs = P("layer", None, None, None, "plane")
    return jax.shard_map(body, mesh=mesh, in_specs=in_specs, out_specs=out_specs, check_vma=False)
```

```python
import jax
import jax.numpy as jnp
from jax import lax
from jax.experimental import pallas as pl
from jax.experimental.pallas import tpu as pltpu
from jax.sharding import PartitionSpec as P


def kernel_mix(source, factor, carried):
    real = source[0] + (factor[0] * carried[0] - factor[1] * carried[1])
    imag = source[1] + (factor[0] * carried[1] + factor[1] * carried[0])
    return real.astype(jnp.bfloat16), imag.astype(jnp.bfloat16)


def kernel_twist(factor, field):
    real = factor[0] * field[0] - factor[1] * field[1]
    imag = factor[0] * field[1] + factor[1] * field[0]
    return real.astype(jnp.bfloat16), imag.astype(jnp.bfloat16)


def kernel_product(rows, inverse):
    count = rows[0].shape[0]
    width = inverse.shape[0]
    flat = jnp.concatenate(rows, axis=0)
    product = jnp.dot(flat, inverse[...], preferred_element_type=jnp.float32)
    real = product[:count, :width] - product[count:, width:]
    imag = product[:count, width:] + product[count:, :width]
    return real, imag


def read(ref):
    return ref[0], ref[1]


def write(ref, pair):
    ref[0] = pair[0]
    ref[1] = pair[1]


def widen(pair):
    return tuple(part.astype(jnp.bfloat16).astype(jnp.float32) for part in pair)


def forward_kernel(single, *refs):
    if single:
        incoming, source, factor, inverse, first_out, outgoing, held, sems = refs
    else:
        (incoming, source, factor, source_next, factor_next, inverse, inverse_next,
         first_out, second_out, outgoing, held, sems) = refs
    copies = [pltpu.make_async_copy(inverse, held.at[0], sems.at[0])]
    if not single:
        copies.append(pltpu.make_async_copy(inverse_next, held.at[1], sems.at[1]))
    for copy in copies:
        copy.start()
    carried = tuple(part.astype(jnp.float32) for part in read(incoming))
    mixed = kernel_mix(read(source), read(factor), carried)
    copies[0].wait()
    first = kernel_product(mixed, held.at[0])
    write(first_out, first)
    if single:
        write(outgoing, tuple(part.astype(jnp.bfloat16) for part in first))
        return
    mixed = kernel_mix(read(source_next), read(factor_next), widen(first))
    copies[1].wait()
    second = kernel_product(mixed, held.at[1])
    write(second_out, second)
    write(outgoing, tuple(part.astype(jnp.bfloat16) for part in second))


def quad_kernel(skip, incoming, *refs):
    stores, factors, inverses = refs[0:4], refs[4:8], refs[8:12]
    sweeps, outgoing, held, sems = refs[12:16], refs[16], refs[17], refs[18]
    order = [2, 1, 0] if skip else [3, 2, 1, 0]
    copies = {i: pltpu.make_async_copy(inverses[i], held.at[i], sems.at[i]) for i in order}
    for panel in order[:2]:
        copies[panel].start()
    queued = 2
    carried = read(incoming)
    for panel in (3, 2, 1, 0):
        store = read(stores[panel])
        if skip and panel == 3:
            sweep = store
        else:
            copies[panel].wait()
            if queued < len(order):
                copies[order[queued]].start()
                queued += 1
            product = kernel_product(carried, held.at[panel])
            sweep = (store[0] + product[0], store[1] + product[1])
        write(sweeps[panel], sweep)
        carried = kernel_twist(read(factors[panel]), sweep)
    write(outgoing, carried)


def quad_call(skip, args, shape, width):
    local = pl.BlockSpec(memory_space=pltpu.VMEM)
    remote = pl.BlockSpec(memory_space=pl.ANY)
    rows = 2 * shape[0] * shape[1]
    matmuls = 3 if skip else 4
    out_shape = [jax.ShapeDtypeStruct(shape, jnp.float32)] * 4
    out_shape.append(jax.ShapeDtypeStruct(shape, jnp.bfloat16))
    return pl.pallas_call(
        lambda *refs: quad_kernel(skip, *refs),
        out_shape=tuple(out_shape),
        in_specs=[local] * 9 + [remote] * 4,
        out_specs=tuple([local] * 5),
        scratch_shapes=[pltpu.VMEM((4, width, 2 * width), jnp.bfloat16),
                        pltpu.SemaphoreType.DMA((4,))],
        compiler_params=pltpu.CompilerParams(vmem_limit_bytes=56 * 1024 * 1024),
        cost_estimate=pl.CostEstimate(
            flops=matmuls * 2 * rows * width * 2 * width, transcendentals=0,
            bytes_accessed=matmuls * width * 2 * width * 2 + 14 * rows * width * 4),
    )(*args)


def pair_call(kernel, args, shape, width, matmuls, remotes, results):
    local = pl.BlockSpec(memory_space=pltpu.VMEM)
    remote = pl.BlockSpec(memory_space=pl.ANY)
    rows = 2 * shape[0] * shape[1]
    out_shape = [jax.ShapeDtypeStruct(shape, jnp.float32)] * (results - 1)
    out_shape.append(jax.ShapeDtypeStruct(shape, jnp.bfloat16))
    return pl.pallas_call(
        kernel,
        out_shape=tuple(out_shape),
        in_specs=[local] * (len(args) - remotes) + [remote] * remotes,
        out_specs=tuple([local] * results),
        scratch_shapes=[pltpu.VMEM((2, width, 2 * width), jnp.bfloat16),
                        pltpu.SemaphoreType.DMA((2,))],
        compiler_params=pltpu.CompilerParams(vmem_limit_bytes=48 * 1024 * 1024),
        cost_estimate=pl.CostEstimate(
            flops=matmuls * 2 * rows * width * 2 * width, transcendentals=0,
            bytes_accessed=matmuls * width * 2 * width * 2 + 8 * rows * width * 4),
    )(*args)


def body(rhs_field, panel_inverse, coupling):
    planes = lax.axis_size("plane")
    layers = lax.axis_size("layer")
    place = lax.axis_index("layer")
    plane = lax.axis_index("plane")
    pairs = layers // 2

    block = rhs_field[0]
    parts, loads, ys, chunk = block.shape
    block = block.reshape(parts, loads, planes, ys // planes, chunk)
    block = jnp.moveaxis(block, 2, 0)
    block = lax.all_to_all(block, "plane", split_axis=0, concat_axis=0, tiled=True)
    lines = jnp.moveaxis(block, 0, 3).reshape(parts, loads * ys // planes, planes * chunk)
    shape = lines.shape

    inverse = panel_inverse[0]
    width = inverse.shape[0]
    factors = jnp.broadcast_to(coupling[0].reshape(parts, shape[1], 1), shape)
    down = [(2 * j + 1, 2 * j) for j in range(pairs)]

    rows = width // planes
    piece = lax.dynamic_slice_in_dim(inverse, plane * rows, rows, 0)
    own_piece = piece
    piece = lax.ppermute(piece, "layer", down)
    inverse_next = lax.all_gather(piece, "plane", axis=0, tiled=True)
    lines_next = lax.ppermute(lines, "layer", down)
    factors_next = lax.ppermute(factors, "layer", down)
    quads = layers // 4
    gather = [(4 * j + 2, 4 * j) for j in range(quads)]
    early = list(range(quads // 2))
    late = list(range(quads // 2, quads))

    def quad_moves(piece, groups):
        return [lax.ppermute(piece, "layer", [(4 * j + offset, 4 * j) for j in groups]) for offset in (2, 3)]

    _, late_piece = lax.optimization_barrier((inverse_next, own_piece))
    late_moved = quad_moves(late_piece, late)
    quad_factors = [lax.ppermute(factor, "layer", gather) for factor in (factors, factors_next)]

    zero = jnp.zeros(shape, jnp.float32)
    outgoing = jnp.zeros(shape, jnp.bfloat16)
    store_a, store_b = zero, zero
    for panel in range(2):
        if panel > 0:
            incoming = lax.ppermute(outgoing, "layer", [(panel - 1, panel)])
        else:
            incoming = outgoing

        def active(incoming, store_a, outgoing):
            kernel = lambda *refs: forward_kernel(True, *refs)
            return pair_call(kernel, (incoming, lines, factors, inverse), shape, width, 1, 1, 2)

        def idle(incoming, store_a, outgoing):
            return store_a, outgoing

        store_a, outgoing = lax.cond(place == panel, active, idle, incoming, store_a, outgoing)
    store_b = lax.ppermute(store_a, "layer", [(1, 0)])

    for section in range(1, pairs):
        source = 1 if section == 1 else 2 * section - 2
        incoming = lax.ppermute(outgoing, "layer", [(source, 2 * section)])
        if section == 2:
            incoming, *late_moved = lax.optimization_barrier((incoming, *late_moved))
        if section == 2 * len(early):
            incoming, early_piece = lax.optimization_barrier((incoming, own_piece))
            early_moved = quad_moves(early_piece, early)

        def active(incoming, store_a, store_b, outgoing):
            kernel = lambda *refs: forward_kernel(False, *refs)
            args = (incoming, lines, factors, lines_next, factors_next, inverse, inverse_next)
            return pair_call(kernel, args, shape, width, 2, 2, 3)

        def idle(incoming, store_a, store_b, outgoing):
            return store_a, store_b, outgoing

        store_a, store_b, outgoing = lax.cond(
            place == 2 * section, active, idle, incoming, store_a, store_b, outgoing)

    is_early = place < 4 * len(early)
    quad_inverses = [lax.all_gather(jnp.where(is_early, first, second), "plane", axis=0, tiled=True)
                     for first, second in zip(early_moved, late_moved)]
    quad_stores = [lax.ppermute(store, "layer", gather) for store in (store_a, store_b)]

    sweeps = (zero, zero, zero, zero)
    for section in range(quads):
        lead = layers - 4 - 4 * section
        if section > 0:
            incoming = lax.ppermute(outgoing, "layer", [(lead + 4, lead)])
        else:
            incoming = outgoing

        def active(incoming, sweeps, outgoing, skip=(section == 0)):
            args = ((incoming, store_a, store_b) + tuple(quad_stores) + (factors, factors_next)
                    + tuple(quad_factors) + (inverse, inverse_next) + tuple(quad_inverses))
            results = quad_call(skip, args, shape, width)
            return tuple(results[:4]), results[4]

        def idle(incoming, sweeps, outgoing):
            return sweeps, outgoing

        sweeps, outgoing = lax.cond(place == lead, active, idle, incoming, sweeps, outgoing)

    result = sweeps[0]
    for offset in (1, 2, 3):
        returned = lax.ppermute(sweeps[offset], "layer", [(4 * j, 4 * j + offset) for j in range(quads)])
        result = jnp.where(place % 4 == offset, returned, result)

    result = result.reshape(parts, loads, ys // planes, planes, chunk)
    result = jnp.moveaxis(result, 3, 0)
    result = lax.all_to_all(result, "plane", split_axis=0, concat_axis=0, tiled=True)
    result = jnp.moveaxis(result, 0, 2).reshape(parts, loads, ys, chunk)
    return result[None]


def solution(mesh):
    in_specs = (
        P("layer", None, None, None, "plane"),
        P("layer", None, None),
        P("layer", None, None, "plane"),
    )
    out_specs = P("layer", None, None, None, "plane")
    return jax.shard_map(body, mesh=mesh, in_specs=in_specs, out_specs=out_specs, check_vma=False)
```

```python
import jax
import jax.numpy as jnp
from jax import lax
from jax.experimental import pallas as pl
from jax.experimental.pallas import tpu as pltpu
from jax.sharding import PartitionSpec as P


def kernel_mix(source, factor, carried):
    real = source[0] + (factor[0] * carried[0] - factor[1] * carried[1])
    imag = source[1] + (factor[0] * carried[1] + factor[1] * carried[0])
    return real.astype(jnp.bfloat16), imag.astype(jnp.bfloat16)


def kernel_twist(factor, field):
    real = factor[0] * field[0] - factor[1] * field[1]
    imag = factor[0] * field[1] + factor[1] * field[0]
    return real.astype(jnp.bfloat16), imag.astype(jnp.bfloat16)


def kernel_product(rows, inverse):
    count = rows[0].shape[0]
    width = inverse.shape[0]
    flat = jnp.concatenate(rows, axis=0)
    product = jnp.dot(flat, inverse[...], preferred_element_type=jnp.float32)
    real = product[:count, :width] - product[count:, width:]
    imag = product[:count, width:] + product[count:, :width]
    return real, imag


def read(ref):
    return ref[0], ref[1]


def write(ref, pair):
    ref[0] = pair[0]
    ref[1] = pair[1]


def widen(pair):
    return tuple(part.astype(jnp.bfloat16).astype(jnp.float32) for part in pair)


def forward_kernel(single, *refs):
    if single:
        incoming, source, factor, inverse, first_out, outgoing, held, sems = refs
    else:
        (incoming, source, factor, source_next, factor_next, inverse, inverse_next,
         first_out, second_out, outgoing, held, sems) = refs
    copies = [pltpu.make_async_copy(inverse, held.at[0], sems.at[0])]
    if not single:
        copies.append(pltpu.make_async_copy(inverse_next, held.at[1], sems.at[1]))
    for copy in copies:
        copy.start()
    carried = tuple(part.astype(jnp.float32) for part in read(incoming))
    mixed = kernel_mix(read(source), read(factor), carried)
    copies[0].wait()
    first = kernel_product(mixed, held.at[0])
    write(first_out, first)
    if single:
        write(outgoing, tuple(part.astype(jnp.bfloat16) for part in first))
        return
    mixed = kernel_mix(read(source_next), read(factor_next), widen(first))
    copies[1].wait()
    second = kernel_product(mixed, held.at[1])
    write(second_out, second)
    write(outgoing, tuple(part.astype(jnp.bfloat16) for part in second))


def quad_forward_kernel(incoming, *refs):
    sources, factors, inverses = refs[0:4], refs[4:8], refs[8:12]
    stores, held, sems = refs[12:16], refs[16], refs[17]
    copies = [pltpu.make_async_copy(inverses[i], held.at[i], sems.at[i]) for i in range(4)]
    for panel in range(2):
        copies[panel].start()
    carried = tuple(part.astype(jnp.float32) for part in read(incoming))
    for panel in range(4):
        mixed = kernel_mix(read(sources[panel]), read(factors[panel]), carried)
        copies[panel].wait()
        if panel + 2 < 4:
            copies[panel + 2].start()
        result = kernel_product(mixed, held.at[panel])
        write(stores[panel], result)
        carried = widen(result)


def quad_forward_call(args, shape, width):
    local = pl.BlockSpec(memory_space=pltpu.VMEM)
    remote = pl.BlockSpec(memory_space=pl.ANY)
    rows = 2 * shape[0] * shape[1]
    return pl.pallas_call(
        quad_forward_kernel,
        out_shape=tuple([jax.ShapeDtypeStruct(shape, jnp.float32)] * 4),
        in_specs=[local] * 9 + [remote] * 4,
        out_specs=tuple([local] * 4),
        scratch_shapes=[pltpu.VMEM((4, width, 2 * width), jnp.bfloat16),
                        pltpu.SemaphoreType.DMA((4,))],
        compiler_params=pltpu.CompilerParams(vmem_limit_bytes=56 * 1024 * 1024),
        cost_estimate=pl.CostEstimate(
            flops=4 * 2 * rows * width * 2 * width, transcendentals=0,
            bytes_accessed=4 * width * 2 * width * 2 + 13 * rows * width * 4),
    )(*args)


def quad_kernel(skip, incoming, *refs):
    stores, factors, inverses = refs[0:4], refs[4:8], refs[8:12]
    sweeps, outgoing, held, sems = refs[12:16], refs[16], refs[17], refs[18]
    order = [2, 1, 0] if skip else [3, 2, 1, 0]
    copies = {i: pltpu.make_async_copy(inverses[i], held.at[i], sems.at[i]) for i in order}
    for panel in order[:2]:
        copies[panel].start()
    queued = 2
    carried = read(incoming)
    for panel in (3, 2, 1, 0):
        store = read(stores[panel])
        if skip and panel == 3:
            sweep = store
        else:
            copies[panel].wait()
            if queued < len(order):
                copies[order[queued]].start()
                queued += 1
            product = kernel_product(carried, held.at[panel])
            sweep = (store[0] + product[0], store[1] + product[1])
        write(sweeps[panel], sweep)
        carried = kernel_twist(read(factors[panel]), sweep)
    write(outgoing, carried)


def quad_call(skip, args, shape, width):
    local = pl.BlockSpec(memory_space=pltpu.VMEM)
    remote = pl.BlockSpec(memory_space=pl.ANY)
    rows = 2 * shape[0] * shape[1]
    matmuls = 3 if skip else 4
    out_shape = [jax.ShapeDtypeStruct(shape, jnp.float32)] * 4
    out_shape.append(jax.ShapeDtypeStruct(shape, jnp.bfloat16))
    return pl.pallas_call(
        lambda *refs: quad_kernel(skip, *refs),
        out_shape=tuple(out_shape),
        in_specs=[local] * 9 + [remote] * 4,
        out_specs=tuple([local] * 5),
        scratch_shapes=[pltpu.VMEM((4, width, 2 * width), jnp.bfloat16),
                        pltpu.SemaphoreType.DMA((4,))],
        compiler_params=pltpu.CompilerParams(vmem_limit_bytes=56 * 1024 * 1024),
        cost_estimate=pl.CostEstimate(
            flops=matmuls * 2 * rows * width * 2 * width, transcendentals=0,
            bytes_accessed=matmuls * width * 2 * width * 2 + 14 * rows * width * 4),
    )(*args)


def pair_call(kernel, args, shape, width, matmuls, remotes, results):
    local = pl.BlockSpec(memory_space=pltpu.VMEM)
    remote = pl.BlockSpec(memory_space=pl.ANY)
    rows = 2 * shape[0] * shape[1]
    out_shape = [jax.ShapeDtypeStruct(shape, jnp.float32)] * (results - 1)
    out_shape.append(jax.ShapeDtypeStruct(shape, jnp.bfloat16))
    return pl.pallas_call(
        kernel,
        out_shape=tuple(out_shape),
        in_specs=[local] * (len(args) - remotes) + [remote] * remotes,
        out_specs=tuple([local] * results),
        scratch_shapes=[pltpu.VMEM((2, width, 2 * width), jnp.bfloat16),
                        pltpu.SemaphoreType.DMA((2,))],
        compiler_params=pltpu.CompilerParams(vmem_limit_bytes=48 * 1024 * 1024),
        cost_estimate=pl.CostEstimate(
            flops=matmuls * 2 * rows * width * 2 * width, transcendentals=0,
            bytes_accessed=matmuls * width * 2 * width * 2 + 8 * rows * width * 4),
    )(*args)


def body(rhs_field, panel_inverse, coupling):
    planes = lax.axis_size("plane")
    layers = lax.axis_size("layer")
    place = lax.axis_index("layer")
    plane = lax.axis_index("plane")
    pairs = layers // 2

    block = rhs_field[0]
    parts, loads, ys, chunk = block.shape
    block = block.reshape(parts, loads, planes, ys // planes, chunk)
    block = jnp.moveaxis(block, 2, 0)
    block = lax.all_to_all(block, "plane", split_axis=0, concat_axis=0, tiled=True)
    lines = jnp.moveaxis(block, 0, 3).reshape(parts, loads * ys // planes, planes * chunk)
    shape = lines.shape

    inverse = panel_inverse[0]
    width = inverse.shape[0]
    factors = jnp.broadcast_to(coupling[0].reshape(parts, shape[1], 1), shape)
    down = [(2 * j + 1, 2 * j) for j in range(pairs)]

    rows = width // planes
    piece = lax.dynamic_slice_in_dim(inverse, plane * rows, rows, 0)
    own_piece = piece
    piece = lax.ppermute(piece, "layer", down)
    inverse_next = lax.all_gather(piece, "plane", axis=0, tiled=True)
    lines_next = lax.ppermute(lines, "layer", down)
    factors_next = lax.ppermute(factors, "layer", down)
    quads = layers // 4
    gather = [(4 * j + 2, 4 * j) for j in range(quads)]
    quad_factors = [lax.ppermute(factor, "layer", gather) for factor in (factors, factors_next)]
    last = layers - 4
    quad_lines = [lax.ppermute(source, "layer", [(last + 2, last)]) for source in (lines, lines_next)]

    zero = jnp.zeros(shape, jnp.float32)
    outgoing = jnp.zeros(shape, jnp.bfloat16)
    store_a, store_b = zero, zero
    for panel in range(2):
        if panel > 0:
            incoming = lax.ppermute(outgoing, "layer", [(panel - 1, panel)])
        else:
            incoming = outgoing

        def active(incoming, store_a, outgoing):
            kernel = lambda *refs: forward_kernel(True, *refs)
            return pair_call(kernel, (incoming, lines, factors, inverse), shape, width, 1, 1, 2)

        def idle(incoming, store_a, outgoing):
            return store_a, outgoing

        store_a, outgoing = lax.cond(place == panel, active, idle, incoming, store_a, outgoing)
    store_b = lax.ppermute(store_a, "layer", [(1, 0)])

    for section in range(1, pairs - 2):
        source = 1 if section == 1 else 2 * section - 2
        incoming = lax.ppermute(outgoing, "layer", [(source, 2 * section)])

        def active(incoming, store_a, store_b, outgoing):
            kernel = lambda *refs: forward_kernel(False, *refs)
            args = (incoming, lines, factors, lines_next, factors_next, inverse, inverse_next)
            return pair_call(kernel, args, shape, width, 2, 2, 3)

        def idle(incoming, store_a, store_b, outgoing):
            return store_a, store_b, outgoing

        store_a, store_b, outgoing = lax.cond(
            place == 2 * section, active, idle, incoming, store_a, store_b, outgoing)
        if section == min(7, pairs - 1):
            outgoing, moved = lax.optimization_barrier((outgoing, own_piece))
            quad_inverses = [
                lax.all_gather(lax.ppermute(moved, "layer", [(4 * j + offset, 4 * j) for j in range(quads)]),
                               "plane", axis=0, tiled=True)
                for offset in (2, 3)]

    incoming = lax.ppermute(outgoing, "layer", [(last - 2, last)])

    def active(incoming, store_a, store_b, extra_a, extra_b):
        args = ((incoming, lines, lines_next) + tuple(quad_lines) + (factors, factors_next)
                + tuple(quad_factors) + (inverse, inverse_next) + tuple(quad_inverses))
        return quad_forward_call(args, shape, width)

    def idle(incoming, store_a, store_b, extra_a, extra_b):
        return store_a, store_b, extra_a, extra_b

    store_a, store_b, extra_a, extra_b = lax.cond(
        place == last, active, idle, incoming, store_a, store_b, zero, zero)
    outgoing = jnp.zeros(shape, jnp.bfloat16)
    gather_stores = [(4 * j + 2, 4 * j) for j in range(quads - 1)]
    quad_stores = [jnp.where(place == last, extra, lax.ppermute(store, "layer", gather_stores))
                   for extra, store in ((extra_a, store_a), (extra_b, store_b))]

    sweeps = (zero, zero, zero, zero)
    for section in range(quads):
        lead = layers - 4 - 4 * section
        if section > 0:
            incoming = lax.ppermute(outgoing, "layer", [(lead + 4, lead)])
        else:
            incoming = outgoing

        def active(incoming, sweeps, outgoing, skip=(section == 0)):
            args = ((incoming, store_a, store_b) + tuple(quad_stores) + (factors, factors_next)
                    + tuple(quad_factors) + (inverse, inverse_next) + tuple(quad_inverses))
            results = quad_call(skip, args, shape, width)
            return tuple(results[:4]), results[4]

        def idle(incoming, sweeps, outgoing):
            return sweeps, outgoing

        sweeps, outgoing = lax.cond(place == lead, active, idle, incoming, sweeps, outgoing)

    result = sweeps[0]
    for offset in (1, 2, 3):
        returned = lax.ppermute(sweeps[offset], "layer", [(4 * j, 4 * j + offset) for j in range(quads)])
        result = jnp.where(place % 4 == offset, returned, result)

    result = result.reshape(parts, loads, ys // planes, planes, chunk)
    result = jnp.moveaxis(result, 3, 0)
    result = lax.all_to_all(result, "plane", split_axis=0, concat_axis=0, tiled=True)
    result = jnp.moveaxis(result, 0, 2).reshape(parts, loads, ys, chunk)
    return result[None]


def solution(mesh):
    in_specs = (
        P("layer", None, None, None, "plane"),
        P("layer", None, None),
        P("layer", None, None, "plane"),
    )
    out_specs = P("layer", None, None, None, "plane")
    return jax.shard_map(body, mesh=mesh, in_specs=in_specs, out_specs=out_specs, check_vma=False)
```

```python
import jax
import jax.numpy as jnp
from jax import lax
from jax.experimental import pallas as pl
from jax.experimental.pallas import tpu as pltpu
from jax.sharding import PartitionSpec as P


def kernel_mix(source, factor, carried):
    real = source[0] + (factor[0] * carried[0] - factor[1] * carried[1])
    imag = source[1] + (factor[0] * carried[1] + factor[1] * carried[0])
    return real.astype(jnp.bfloat16), imag.astype(jnp.bfloat16)


def kernel_twist(factor, field):
    real = factor[0] * field[0] - factor[1] * field[1]
    imag = factor[0] * field[1] + factor[1] * field[0]
    return real.astype(jnp.bfloat16), imag.astype(jnp.bfloat16)


def kernel_product(rows, inverse):
    count = rows[0].shape[0]
    width = inverse.shape[0]
    flat = jnp.concatenate(rows, axis=0)
    product = jnp.dot(flat, inverse[...], preferred_element_type=jnp.float32)
    real = product[:count, :width] - product[count:, width:]
    imag = product[:count, width:] + product[count:, :width]
    return real, imag


def read(ref):
    return ref[0], ref[1]


def write(ref, pair):
    ref[0] = pair[0]
    ref[1] = pair[1]


def widen(pair):
    return tuple(part.astype(jnp.bfloat16).astype(jnp.float32) for part in pair)


def forward_kernel(single, *refs):
    if single:
        incoming, source, factor, inverse, first_out, outgoing, held, sems = refs
    else:
        (incoming, source, factor, source_next, factor_next, inverse, inverse_next,
         first_out, second_out, outgoing, held, sems) = refs
    copies = [pltpu.make_async_copy(inverse, held.at[0], sems.at[0])]
    if not single:
        copies.append(pltpu.make_async_copy(inverse_next, held.at[1], sems.at[1]))
    for copy in copies:
        copy.start()
    carried = tuple(part.astype(jnp.float32) for part in read(incoming))
    mixed = kernel_mix(read(source), read(factor), carried)
    copies[0].wait()
    first = kernel_product(mixed, held.at[0])
    write(first_out, first)
    if single:
        write(outgoing, tuple(part.astype(jnp.bfloat16) for part in first))
        return
    mixed = kernel_mix(read(source_next), read(factor_next), widen(first))
    copies[1].wait()
    second = kernel_product(mixed, held.at[1])
    write(second_out, second)
    write(outgoing, tuple(part.astype(jnp.bfloat16) for part in second))


def quad_forward_kernel(incoming, *refs):
    sources, factors, inverses = refs[0:4], refs[4:8], refs[8:12]
    stores, held, sems = refs[12:16], refs[16], refs[17]
    copies = [pltpu.make_async_copy(inverses[i], held.at[i], sems.at[i]) for i in range(4)]
    for panel in range(2):
        copies[panel].start()
    carried = tuple(part.astype(jnp.float32) for part in read(incoming))
    for panel in range(4):
        mixed = kernel_mix(read(sources[panel]), read(factors[panel]), carried)
        copies[panel].wait()
        if panel + 2 < 4:
            copies[panel + 2].start()
        result = kernel_product(mixed, held.at[panel])
        write(stores[panel], result)
        carried = widen(result)


def quad_forward_call(args, shape, width):
    local = pl.BlockSpec(memory_space=pltpu.VMEM)
    remote = pl.BlockSpec(memory_space=pl.ANY)
    rows = 2 * shape[0] * shape[1]
    return pl.pallas_call(
        quad_forward_kernel,
        out_shape=tuple([jax.ShapeDtypeStruct(shape, jnp.float32)] * 4),
        in_specs=[local] * 9 + [remote] * 4,
        out_specs=tuple([local] * 4),
        scratch_shapes=[pltpu.VMEM((4, width, 2 * width), jnp.bfloat16),
                        pltpu.SemaphoreType.DMA((4,))],
        compiler_params=pltpu.CompilerParams(vmem_limit_bytes=56 * 1024 * 1024),
        cost_estimate=pl.CostEstimate(
            flops=4 * 2 * rows * width * 2 * width, transcendentals=0,
            bytes_accessed=4 * width * 2 * width * 2 + 13 * rows * width * 4),
    )(*args)


def quad_kernel(skip, incoming, *refs):
    stores, factors, inverses = refs[0:4], refs[4:8], refs[8:12]
    sweeps, outgoing, held, sems = refs[12:16], refs[16], refs[17], refs[18]
    order = [2, 1, 0] if skip else [3, 2, 1, 0]
    copies = {i: pltpu.make_async_copy(inverses[i], held.at[i], sems.at[i]) for i in order}
    for panel in order[:2]:
        copies[panel].start()
    queued = 2
    carried = read(incoming)
    for panel in (3, 2, 1, 0):
        store = read(stores[panel])
        if skip and panel == 3:
            sweep = store
        else:
            copies[panel].wait()
            if queued < len(order):
                copies[order[queued]].start()
                queued += 1
            product = kernel_product(carried, held.at[panel])
            sweep = (store[0] + product[0], store[1] + product[1])
        write(sweeps[panel], sweep)
        carried = kernel_twist(read(factors[panel]), sweep)
    write(outgoing, carried)


def quad_call(skip, args, shape, width):
    local = pl.BlockSpec(memory_space=pltpu.VMEM)
    remote = pl.BlockSpec(memory_space=pl.ANY)
    rows = 2 * shape[0] * shape[1]
    matmuls = 3 if skip else 4
    out_shape = [jax.ShapeDtypeStruct(shape, jnp.float32)] * 4
    out_shape.append(jax.ShapeDtypeStruct(shape, jnp.bfloat16))
    return pl.pallas_call(
        lambda *refs: quad_kernel(skip, *refs),
        out_shape=tuple(out_shape),
        in_specs=[local] * 9 + [remote] * 4,
        out_specs=tuple([local] * 5),
        scratch_shapes=[pltpu.VMEM((4, width, 2 * width), jnp.bfloat16),
                        pltpu.SemaphoreType.DMA((4,))],
        compiler_params=pltpu.CompilerParams(vmem_limit_bytes=56 * 1024 * 1024),
        cost_estimate=pl.CostEstimate(
            flops=matmuls * 2 * rows * width * 2 * width, transcendentals=0,
            bytes_accessed=matmuls * width * 2 * width * 2 + 14 * rows * width * 4),
    )(*args)


def pair_call(kernel, args, shape, width, matmuls, remotes, results):
    local = pl.BlockSpec(memory_space=pltpu.VMEM)
    remote = pl.BlockSpec(memory_space=pl.ANY)
    rows = 2 * shape[0] * shape[1]
    out_shape = [jax.ShapeDtypeStruct(shape, jnp.float32)] * (results - 1)
    out_shape.append(jax.ShapeDtypeStruct(shape, jnp.bfloat16))
    return pl.pallas_call(
        kernel,
        out_shape=tuple(out_shape),
        in_specs=[local] * (len(args) - remotes) + [remote] * remotes,
        out_specs=tuple([local] * results),
        scratch_shapes=[pltpu.VMEM((2, width, 2 * width), jnp.bfloat16),
                        pltpu.SemaphoreType.DMA((2,))],
        compiler_params=pltpu.CompilerParams(vmem_limit_bytes=48 * 1024 * 1024),
        cost_estimate=pl.CostEstimate(
            flops=matmuls * 2 * rows * width * 2 * width, transcendentals=0,
            bytes_accessed=matmuls * width * 2 * width * 2 + 8 * rows * width * 4),
    )(*args)


def body(rhs_field, panel_inverse, coupling):
    planes = lax.axis_size("plane")
    layers = lax.axis_size("layer")
    place = lax.axis_index("layer")
    plane = lax.axis_index("plane")
    pairs = layers // 2

    block = rhs_field[0]
    parts, loads, ys, chunk = block.shape
    block = block.reshape(parts, loads, planes, ys // planes, chunk)
    block = jnp.moveaxis(block, 2, 0)
    block = lax.all_to_all(block, "plane", split_axis=0, concat_axis=0, tiled=True)
    lines = jnp.moveaxis(block, 0, 3).reshape(parts, loads * ys // planes, planes * chunk)
    shape = lines.shape

    inverse = panel_inverse[0]
    width = inverse.shape[0]
    factors = jnp.broadcast_to(coupling[0].reshape(parts, shape[1], 1), shape)
    down = [(2 * j + 1, 2 * j) for j in range(pairs)]

    rows = width // planes
    piece = lax.dynamic_slice_in_dim(inverse, plane * rows, rows, 0)
    own_piece = piece
    piece = lax.ppermute(piece, "layer", down)
    inverse_next = lax.all_gather(piece, "plane", axis=0, tiled=True)
    lines_next = lax.ppermute(lines, "layer", down)
    factors_next = lax.ppermute(factors, "layer", down)
    quads = layers // 4
    gather = [(4 * j + 2, 4 * j) for j in range(quads)]
    quad_factors = [lax.ppermute(factor, "layer", gather) for factor in (factors, factors_next)]
    last = layers - 4
    tie = 7
    boundary = (tie - 1) // 2

    def quad_moves(piece, groups):
        return [lax.ppermute(piece, "layer", [(4 * j + offset, 4 * j) for j in groups]) for offset in (2, 3)]

    quad_lines = [lax.ppermute(source, "layer", [(last + 2, last)]) for source in (lines, lines_next)]

    zero = jnp.zeros(shape, jnp.float32)
    outgoing = jnp.zeros(shape, jnp.bfloat16)
    store_a, store_b = zero, zero
    for panel in range(2):
        if panel > 0:
            incoming = lax.ppermute(outgoing, "layer", [(panel - 1, panel)])
        else:
            incoming = outgoing

        def active(incoming, store_a, outgoing):
            kernel = lambda *refs: forward_kernel(True, *refs)
            return pair_call(kernel, (incoming, lines, factors, inverse), shape, width, 1, 1, 2)

        def idle(incoming, store_a, outgoing):
            return store_a, outgoing

        store_a, outgoing = lax.cond(place == panel, active, idle, incoming, store_a, outgoing)
    store_b = lax.ppermute(store_a, "layer", [(1, 0)])

    for section in range(1, pairs - 2):
        source = 1 if section == 1 else 2 * section - 2
        if section == tie + 1:
            outgoing, *main_moved = lax.optimization_barrier((outgoing, *main_moved))
        incoming = lax.ppermute(outgoing, "layer", [(source, 2 * section)])
        if section == tie + 1:
            incoming, moved = lax.optimization_barrier((incoming, own_piece))
            boundary_moved = quad_moves(moved, [boundary])

        def active(incoming, store_a, store_b, outgoing):
            kernel = lambda *refs: forward_kernel(False, *refs)
            args = (incoming, lines, factors, lines_next, factors_next, inverse, inverse_next)
            return pair_call(kernel, args, shape, width, 2, 2, 3)

        def idle(incoming, store_a, store_b, outgoing):
            return store_a, store_b, outgoing

        store_a, store_b, outgoing = lax.cond(
            place == 2 * section, active, idle, incoming, store_a, store_b, outgoing)
        if section == tie:
            outgoing, moved = lax.optimization_barrier((outgoing, own_piece))
            main_moved = quad_moves(moved, [j for j in range(quads) if j != boundary])

    quad_inverses = [lax.all_gather(jnp.where(place == 4 * boundary, second, first), "plane", axis=0, tiled=True)
                     for first, second in zip(main_moved, boundary_moved)]
    incoming = lax.ppermute(outgoing, "layer", [(last - 2, last)])

    def active(incoming, store_a, store_b, extra_a, extra_b):
        args = ((incoming, lines, lines_next) + tuple(quad_lines) + (factors, factors_next)
                + tuple(quad_factors) + (inverse, inverse_next) + tuple(quad_inverses))
        return quad_forward_call(args, shape, width)

    def idle(incoming, store_a, store_b, extra_a, extra_b):
        return store_a, store_b, extra_a, extra_b

    store_a, store_b, extra_a, extra_b = lax.cond(
        place == last, active, idle, incoming, store_a, store_b, zero, zero)
    outgoing = jnp.zeros(shape, jnp.bfloat16)
    gather_stores = [(4 * j + 2, 4 * j) for j in range(quads - 1)]
    quad_stores = [jnp.where(place == last, extra, lax.ppermute(store, "layer", gather_stores))
                   for extra, store in ((extra_a, store_a), (extra_b, store_b))]

    sweeps = (zero, zero, zero, zero)
    for section in range(quads):
        lead = layers - 4 - 4 * section
        if section > 0:
            incoming = lax.ppermute(outgoing, "layer", [(lead + 4, lead)])
        else:
            incoming = outgoing

        def active(incoming, sweeps, outgoing, skip=(section == 0)):
            args = ((incoming, store_a, store_b) + tuple(quad_stores) + (factors, factors_next)
                    + tuple(quad_factors) + (inverse, inverse_next) + tuple(quad_inverses))
            results = quad_call(skip, args, shape, width)
            return tuple(results[:4]), results[4]

        def idle(incoming, sweeps, outgoing):
            return sweeps, outgoing

        sweeps, outgoing = lax.cond(place == lead, active, idle, incoming, sweeps, outgoing)

    result = sweeps[0]
    for offset in (1, 2, 3):
        returned = lax.ppermute(sweeps[offset], "layer", [(4 * j, 4 * j + offset) for j in range(quads)])
        result = jnp.where(place % 4 == offset, returned, result)

    result = result.reshape(parts, loads, ys // planes, planes, chunk)
    result = jnp.moveaxis(result, 3, 0)
    result = lax.all_to_all(result, "plane", split_axis=0, concat_axis=0, tiled=True)
    result = jnp.moveaxis(result, 0, 2).reshape(parts, loads, ys, chunk)
    return result[None]


def solution(mesh):
    in_specs = (
        P("layer", None, None, None, "plane"),
        P("layer", None, None),
        P("layer", None, None, "plane"),
    )
    out_specs = P("layer", None, None, None, "plane")
    return jax.shard_map(body, mesh=mesh, in_specs=in_specs, out_specs=out_specs, check_vma=False)
```

```python
import jax
import jax.numpy as jnp
from jax import lax
from jax.experimental import pallas as pl
from jax.experimental.pallas import tpu as pltpu
from jax.sharding import PartitionSpec as P


def kernel_mix(source, factor, carried):
    real = source[0] + (factor[0] * carried[0] - factor[1] * carried[1])
    imag = source[1] + (factor[0] * carried[1] + factor[1] * carried[0])
    return real.astype(jnp.bfloat16), imag.astype(jnp.bfloat16)


def kernel_twist(factor, field):
    real = factor[0] * field[0] - factor[1] * field[1]
    imag = factor[0] * field[1] + factor[1] * field[0]
    return real.astype(jnp.bfloat16), imag.astype(jnp.bfloat16)


CHUNKS = 4


def chunk_copies(inverse, slot, sems):
    width = inverse.shape[0]
    part = width // CHUNKS
    copies = []
    for chunk in range(CHUNKS):
        for half in range(2):
            copies.append(pltpu.make_async_copy(
                inverse.at[:, pl.ds(half * width + chunk * part, part)],
                slot.at[chunk, :, pl.ds(half * part, part)],
                sems.at[chunk, half]))
    return copies


def kernel_product(rows, slot, copies):
    count = rows[0].shape[0]
    part = slot.shape[2] // 2
    flat = jnp.concatenate(rows, axis=0)
    reals, imags = [], []
    for chunk in range(CHUNKS):
        copies[2 * chunk].wait()
        copies[2 * chunk + 1].wait()
        product = jnp.dot(flat, slot[chunk], preferred_element_type=jnp.float32)
        reals.append(product[:count, :part] - product[count:, part:])
        imags.append(product[:count, part:] + product[count:, :part])
    return jnp.concatenate(reals, axis=1), jnp.concatenate(imags, axis=1)


def start(copies):
    for copy in copies:
        copy.start()


def read(ref):
    return ref[0], ref[1]


def write(ref, pair):
    ref[0] = pair[0]
    ref[1] = pair[1]


def widen(pair):
    return tuple(part.astype(jnp.bfloat16).astype(jnp.float32) for part in pair)


def forward_kernel(single, *refs):
    if single:
        incoming, source, factor, inverse, first_out, outgoing, held, sems = refs
    else:
        (incoming, source, factor, source_next, factor_next, inverse, inverse_next,
         first_out, second_out, outgoing, held, sems) = refs
    copies = [chunk_copies(inverse, held.at[0], sems.at[0])]
    if not single:
        copies.append(chunk_copies(inverse_next, held.at[1], sems.at[1]))
    for group in copies:
        start(group)
    carried = tuple(part.astype(jnp.float32) for part in read(incoming))
    mixed = kernel_mix(read(source), read(factor), carried)
    first = kernel_product(mixed, held.at[0], copies[0])
    write(first_out, first)
    if single:
        write(outgoing, tuple(part.astype(jnp.bfloat16) for part in first))
        return
    mixed = kernel_mix(read(source_next), read(factor_next), widen(first))
    second = kernel_product(mixed, held.at[1], copies[1])
    write(second_out, second)
    write(outgoing, tuple(part.astype(jnp.bfloat16) for part in second))


def quad_forward_kernel(incoming, *refs):
    sources, factors, inverses = refs[0:4], refs[4:8], refs[8:12]
    stores, held, sems = refs[12:16], refs[16], refs[17]
    copies = [chunk_copies(inverses[i], held.at[i], sems.at[i]) for i in range(4)]
    for panel in range(2):
        start(copies[panel])
    carried = tuple(part.astype(jnp.float32) for part in read(incoming))
    for panel in range(4):
        mixed = kernel_mix(read(sources[panel]), read(factors[panel]), carried)
        result = kernel_product(mixed, held.at[panel], copies[panel])
        if panel + 2 < 4:
            start(copies[panel + 2])
        write(stores[panel], result)
        carried = widen(result)


def quad_forward_call(args, shape, width):
    local = pl.BlockSpec(memory_space=pltpu.VMEM)
    remote = pl.BlockSpec(memory_space=pl.ANY)
    rows = 2 * shape[0] * shape[1]
    return pl.pallas_call(
        quad_forward_kernel,
        out_shape=tuple([jax.ShapeDtypeStruct(shape, jnp.float32)] * 4),
        in_specs=[local] * 9 + [remote] * 4,
        out_specs=tuple([local] * 4),
        scratch_shapes=[pltpu.VMEM((4, CHUNKS, width, 2 * width // CHUNKS), jnp.bfloat16),
                        pltpu.SemaphoreType.DMA((4, CHUNKS, 2))],
        compiler_params=pltpu.CompilerParams(vmem_limit_bytes=56 * 1024 * 1024),
        cost_estimate=pl.CostEstimate(
            flops=4 * 2 * rows * width * 2 * width, transcendentals=0,
            bytes_accessed=4 * width * 2 * width * 2 + 13 * rows * width * 4),
    )(*args)


def quad_kernel(skip, incoming, *refs):
    stores, factors, inverses = refs[0:4], refs[4:8], refs[8:12]
    sweeps, outgoing, held, sems = refs[12:16], refs[16], refs[17], refs[18]
    order = [2, 1, 0] if skip else [3, 2, 1, 0]
    copies = {i: chunk_copies(inverses[i], held.at[i], sems.at[i]) for i in order}
    for panel in order[:2]:
        start(copies[panel])
    queued = 2
    carried = read(incoming)
    for panel in (3, 2, 1, 0):
        store = read(stores[panel])
        if skip and panel == 3:
            sweep = store
        else:
            product = kernel_product(carried, held.at[panel], copies[panel])
            if queued < len(order):
                start(copies[order[queued]])
                queued += 1
            sweep = (store[0] + product[0], store[1] + product[1])
        write(sweeps[panel], sweep)
        carried = kernel_twist(read(factors[panel]), sweep)
    write(outgoing, carried)


def quad_call(skip, args, shape, width):
    local = pl.BlockSpec(memory_space=pltpu.VMEM)
    remote = pl.BlockSpec(memory_space=pl.ANY)
    rows = 2 * shape[0] * shape[1]
    matmuls = 3 if skip else 4
    out_shape = [jax.ShapeDtypeStruct(shape, jnp.float32)] * 4
    out_shape.append(jax.ShapeDtypeStruct(shape, jnp.bfloat16))
    return pl.pallas_call(
        lambda *refs: quad_kernel(skip, *refs),
        out_shape=tuple(out_shape),
        in_specs=[local] * 9 + [remote] * 4,
        out_specs=tuple([local] * 5),
        scratch_shapes=[pltpu.VMEM((4, CHUNKS, width, 2 * width // CHUNKS), jnp.bfloat16),
                        pltpu.SemaphoreType.DMA((4, CHUNKS, 2))],
        compiler_params=pltpu.CompilerParams(vmem_limit_bytes=56 * 1024 * 1024),
        cost_estimate=pl.CostEstimate(
            flops=matmuls * 2 * rows * width * 2 * width, transcendentals=0,
            bytes_accessed=matmuls * width * 2 * width * 2 + 14 * rows * width * 4),
    )(*args)


def pair_call(kernel, args, shape, width, matmuls, remotes, results):
    local = pl.BlockSpec(memory_space=pltpu.VMEM)
    remote = pl.BlockSpec(memory_space=pl.ANY)
    rows = 2 * shape[0] * shape[1]
    out_shape = [jax.ShapeDtypeStruct(shape, jnp.float32)] * (results - 1)
    out_shape.append(jax.ShapeDtypeStruct(shape, jnp.bfloat16))
    return pl.pallas_call(
        kernel,
        out_shape=tuple(out_shape),
        in_specs=[local] * (len(args) - remotes) + [remote] * remotes,
        out_specs=tuple([local] * results),
        scratch_shapes=[pltpu.VMEM((2, CHUNKS, width, 2 * width // CHUNKS), jnp.bfloat16),
                        pltpu.SemaphoreType.DMA((2, CHUNKS, 2))],
        compiler_params=pltpu.CompilerParams(vmem_limit_bytes=48 * 1024 * 1024),
        cost_estimate=pl.CostEstimate(
            flops=matmuls * 2 * rows * width * 2 * width, transcendentals=0,
            bytes_accessed=matmuls * width * 2 * width * 2 + 8 * rows * width * 4),
    )(*args)


def body(rhs_field, panel_inverse, coupling):
    planes = lax.axis_size("plane")
    layers = lax.axis_size("layer")
    place = lax.axis_index("layer")
    plane = lax.axis_index("plane")
    pairs = layers // 2

    block = rhs_field[0]
    parts, loads, ys, chunk = block.shape
    block = block.reshape(parts, loads, planes, ys // planes, chunk)
    block = jnp.moveaxis(block, 2, 0)
    block = lax.all_to_all(block, "plane", split_axis=0, concat_axis=0, tiled=True)
    lines = jnp.moveaxis(block, 0, 3).reshape(parts, loads * ys // planes, planes * chunk)
    shape = lines.shape

    inverse = panel_inverse[0]
    width = inverse.shape[0]
    factors = jnp.broadcast_to(coupling[0].reshape(parts, shape[1], 1), shape)
    down = [(2 * j + 1, 2 * j) for j in range(pairs)]

    rows = width // planes
    piece = lax.dynamic_slice_in_dim(inverse, plane * rows, rows, 0)
    own_piece = piece
    piece = lax.ppermute(piece, "layer", down)
    inverse_next = lax.all_gather(piece, "plane", axis=0, tiled=True)
    lines_next = lax.ppermute(lines, "layer", down)
    factors_next = lax.ppermute(factors, "layer", down)
    quads = layers // 4
    gather = [(4 * j + 2, 4 * j) for j in range(quads)]
    quad_factors = [lax.ppermute(factor, "layer", gather) for factor in (factors, factors_next)]
    last = layers - 4
    quad_lines = [lax.ppermute(source, "layer", [(last + 2, last)]) for source in (lines, lines_next)]

    zero = jnp.zeros(shape, jnp.float32)
    outgoing = jnp.zeros(shape, jnp.bfloat16)
    store_a, store_b = zero, zero
    for panel in range(2):
        if panel > 0:
            incoming = lax.ppermute(outgoing, "layer", [(panel - 1, panel)])
        else:
            incoming = outgoing

        def active(incoming, store_a, outgoing):
            kernel = lambda *refs: forward_kernel(True, *refs)
            return pair_call(kernel, (incoming, lines, factors, inverse), shape, width, 1, 1, 2)

        def idle(incoming, store_a, outgoing):
            return store_a, outgoing

        store_a, outgoing = lax.cond(place == panel, active, idle, incoming, store_a, outgoing)
    store_b = lax.ppermute(store_a, "layer", [(1, 0)])

    for section in range(1, pairs - 2):
        source = 1 if section == 1 else 2 * section - 2
        incoming = lax.ppermute(outgoing, "layer", [(source, 2 * section)])

        def active(incoming, store_a, store_b, outgoing):
            kernel = lambda *refs: forward_kernel(False, *refs)
            args = (incoming, lines, factors, lines_next, factors_next, inverse, inverse_next)
            return pair_call(kernel, args, shape, width, 2, 2, 3)

        def idle(incoming, store_a, store_b, outgoing):
            return store_a, store_b, outgoing

        store_a, store_b, outgoing = lax.cond(
            place == 2 * section, active, idle, incoming, store_a, store_b, outgoing)
        if section == min(7, pairs - 1):
            outgoing, moved = lax.optimization_barrier((outgoing, own_piece))
            quad_inverses = [
                lax.all_gather(lax.ppermute(moved, "layer", [(4 * j + offset, 4 * j) for j in range(quads)]),
                               "plane", axis=0, tiled=True)
                for offset in (2, 3)]

    incoming = lax.ppermute(outgoing, "layer", [(last - 2, last)])

    def active(incoming, store_a, store_b, extra_a, extra_b):
        args = ((incoming, lines, lines_next) + tuple(quad_lines) + (factors, factors_next)
                + tuple(quad_factors) + (inverse, inverse_next) + tuple(quad_inverses))
        return quad_forward_call(args, shape, width)

    def idle(incoming, store_a, store_b, extra_a, extra_b):
        return store_a, store_b, extra_a, extra_b

    store_a, store_b, extra_a, extra_b = lax.cond(
        place == last, active, idle, incoming, store_a, store_b, zero, zero)
    outgoing = jnp.zeros(shape, jnp.bfloat16)
    gather_stores = [(4 * j + 2, 4 * j) for j in range(quads - 1)]
    quad_stores = [jnp.where(place == last, extra, lax.ppermute(store, "layer", gather_stores))
                   for extra, store in ((extra_a, store_a), (extra_b, store_b))]

    sweeps = (zero, zero, zero, zero)
    for section in range(quads):
        lead = layers - 4 - 4 * section
        if section > 0:
            incoming = lax.ppermute(outgoing, "layer", [(lead + 4, lead)])
        else:
            incoming = outgoing

        def active(incoming, sweeps, outgoing, skip=(section == 0)):
            args = ((incoming, store_a, store_b) + tuple(quad_stores) + (factors, factors_next)
                    + tuple(quad_factors) + (inverse, inverse_next) + tuple(quad_inverses))
            results = quad_call(skip, args, shape, width)
            return tuple(results[:4]), results[4]

        def idle(incoming, sweeps, outgoing):
            return sweeps, outgoing

        sweeps, outgoing = lax.cond(place == lead, active, idle, incoming, sweeps, outgoing)

    result = sweeps[0]
    for offset in (1, 2, 3):
        returned = lax.ppermute(sweeps[offset], "layer", [(4 * j, 4 * j + offset) for j in range(quads)])
        result = jnp.where(place % 4 == offset, returned, result)

    result = result.reshape(parts, loads, ys // planes, planes, chunk)
    result = jnp.moveaxis(result, 3, 0)
    result = lax.all_to_all(result, "plane", split_axis=0, concat_axis=0, tiled=True)
    result = jnp.moveaxis(result, 0, 2).reshape(parts, loads, ys, chunk)
    return result[None]


def solution(mesh):
    in_specs = (
        P("layer", None, None, None, "plane"),
        P("layer", None, None),
        P("layer", None, None, "plane"),
    )
    out_specs = P("layer", None, None, None, "plane")
    return jax.shard_map(body, mesh=mesh, in_specs=in_specs, out_specs=out_specs, check_vma=False)
```

```python
import jax
import jax.numpy as jnp
from jax import lax
from jax.experimental import pallas as pl
from jax.experimental.pallas import tpu as pltpu
from jax.sharding import PartitionSpec as P


def kernel_mix(source, factor, carried):
    real = source[0] + (factor[0] * carried[0] - factor[1] * carried[1])
    imag = source[1] + (factor[0] * carried[1] + factor[1] * carried[0])
    return real.astype(jnp.bfloat16), imag.astype(jnp.bfloat16)


def kernel_twist(factor, field):
    real = factor[0] * field[0] - factor[1] * field[1]
    imag = factor[0] * field[1] + factor[1] * field[0]
    return real.astype(jnp.bfloat16), imag.astype(jnp.bfloat16)


def product_into(rows, inverse, out, base=None):
    count = rows[0].shape[0]
    width = inverse.shape[0]
    part = 256
    flat = jnp.concatenate(rows, axis=0)

    def chunk(index, carry):
        low = pl.multiple_of(index * part, part)
        high = pl.multiple_of(width + index * part, part)
        left = jnp.dot(flat, inverse[:, pl.ds(low, part)], preferred_element_type=jnp.float32)
        right = jnp.dot(flat, inverse[:, pl.ds(high, part)], preferred_element_type=jnp.float32)
        real = left[:count] - right[count:]
        imag = right[:count] + left[count:]
        if base is not None:
            real = base[0, :, pl.ds(low, part)] + real
            imag = base[1, :, pl.ds(low, part)] + imag
        out[0, :, pl.ds(low, part)] = real
        out[1, :, pl.ds(low, part)] = imag
        return carry

    lax.fori_loop(0, width // part, chunk, 0)
    return read(out)


def read(ref):
    return ref[0], ref[1]


def write(ref, pair):
    ref[0] = pair[0]
    ref[1] = pair[1]


def widen(pair):
    return tuple(part.astype(jnp.bfloat16).astype(jnp.float32) for part in pair)


def forward_kernel(single, *refs):
    if single:
        incoming, source, factor, inverse, first_out, outgoing, held, sems = refs
    else:
        (incoming, source, factor, source_next, factor_next, inverse, inverse_next,
         first_out, second_out, outgoing, held, sems) = refs
    copies = [pltpu.make_async_copy(inverse, held.at[0], sems.at[0])]
    if not single:
        copies.append(pltpu.make_async_copy(inverse_next, held.at[1], sems.at[1]))
    for copy in copies:
        copy.start()
    carried = tuple(part.astype(jnp.float32) for part in read(incoming))
    mixed = kernel_mix(read(source), read(factor), carried)
    copies[0].wait()
    first = product_into(mixed, held.at[0], first_out)
    if single:
        write(outgoing, tuple(part.astype(jnp.bfloat16) for part in first))
        return
    mixed = kernel_mix(read(source_next), read(factor_next), widen(first))
    copies[1].wait()
    second = product_into(mixed, held.at[1], second_out)
    write(outgoing, tuple(part.astype(jnp.bfloat16) for part in second))


def quad_forward_kernel(incoming, *refs):
    sources, factors, inverses = refs[0:4], refs[4:8], refs[8:12]
    stores, held, sems = refs[12:16], refs[16], refs[17]
    copies = [pltpu.make_async_copy(inverses[i], held.at[i], sems.at[i]) for i in range(4)]
    for panel in range(2):
        copies[panel].start()
    carried = tuple(part.astype(jnp.float32) for part in read(incoming))
    for panel in range(4):
        mixed = kernel_mix(read(sources[panel]), read(factors[panel]), carried)
        copies[panel].wait()
        if panel + 2 < 4:
            copies[panel + 2].start()
        result = product_into(mixed, held.at[panel], stores[panel])
        carried = widen(result)


def quad_forward_call(args, shape, width):
    local = pl.BlockSpec(memory_space=pltpu.VMEM)
    remote = pl.BlockSpec(memory_space=pl.ANY)
    rows = 2 * shape[0] * shape[1]
    return pl.pallas_call(
        quad_forward_kernel,
        out_shape=tuple([jax.ShapeDtypeStruct(shape, jnp.float32)] * 4),
        in_specs=[local] * 9 + [remote] * 4,
        out_specs=tuple([local] * 4),
        scratch_shapes=[pltpu.VMEM((4, width, 2 * width), jnp.bfloat16),
                        pltpu.SemaphoreType.DMA((4,))],
        compiler_params=pltpu.CompilerParams(vmem_limit_bytes=56 * 1024 * 1024),
        cost_estimate=pl.CostEstimate(
            flops=4 * 2 * rows * width * 2 * width, transcendentals=0,
            bytes_accessed=4 * width * 2 * width * 2 + 13 * rows * width * 4),
    )(*args)


def quad_kernel(skip, incoming, *refs):
    stores, factors, inverses = refs[0:4], refs[4:8], refs[8:12]
    sweeps, outgoing, held, sems = refs[12:16], refs[16], refs[17], refs[18]
    order = [2, 1, 0] if skip else [3, 2, 1, 0]
    copies = {i: pltpu.make_async_copy(inverses[i], held.at[i], sems.at[i]) for i in order}
    for panel in order[:2]:
        copies[panel].start()
    queued = 2
    carried = read(incoming)
    for panel in (3, 2, 1, 0):
        if skip and panel == 3:
            sweep = read(stores[panel])
            write(sweeps[panel], sweep)
        else:
            copies[panel].wait()
            if queued < len(order):
                copies[order[queued]].start()
                queued += 1
            sweep = product_into(carried, held.at[panel], sweeps[panel], stores[panel])
        carried = kernel_twist(read(factors[panel]), sweep)
    write(outgoing, carried)


def quad_call(skip, args, shape, width):
    local = pl.BlockSpec(memory_space=pltpu.VMEM)
    remote = pl.BlockSpec(memory_space=pl.ANY)
    rows = 2 * shape[0] * shape[1]
    matmuls = 3 if skip else 4
    out_shape = [jax.ShapeDtypeStruct(shape, jnp.float32)] * 4
    out_shape.append(jax.ShapeDtypeStruct(shape, jnp.bfloat16))
    return pl.pallas_call(
        lambda *refs: quad_kernel(skip, *refs),
        out_shape=tuple(out_shape),
        in_specs=[local] * 9 + [remote] * 4,
        out_specs=tuple([local] * 5),
        scratch_shapes=[pltpu.VMEM((4, width, 2 * width), jnp.bfloat16),
                        pltpu.SemaphoreType.DMA((4,))],
        compiler_params=pltpu.CompilerParams(vmem_limit_bytes=56 * 1024 * 1024),
        cost_estimate=pl.CostEstimate(
            flops=matmuls * 2 * rows * width * 2 * width, transcendentals=0,
            bytes_accessed=matmuls * width * 2 * width * 2 + 14 * rows * width * 4),
    )(*args)


def pair_call(kernel, args, shape, width, matmuls, remotes, results):
    local = pl.BlockSpec(memory_space=pltpu.VMEM)
    remote = pl.BlockSpec(memory_space=pl.ANY)
    rows = 2 * shape[0] * shape[1]
    out_shape = [jax.ShapeDtypeStruct(shape, jnp.float32)] * (results - 1)
    out_shape.append(jax.ShapeDtypeStruct(shape, jnp.bfloat16))
    return pl.pallas_call(
        kernel,
        out_shape=tuple(out_shape),
        in_specs=[local] * (len(args) - remotes) + [remote] * remotes,
        out_specs=tuple([local] * results),
        scratch_shapes=[pltpu.VMEM((2, width, 2 * width), jnp.bfloat16),
                        pltpu.SemaphoreType.DMA((2,))],
        compiler_params=pltpu.CompilerParams(vmem_limit_bytes=48 * 1024 * 1024),
        cost_estimate=pl.CostEstimate(
            flops=matmuls * 2 * rows * width * 2 * width, transcendentals=0,
            bytes_accessed=matmuls * width * 2 * width * 2 + 8 * rows * width * 4),
    )(*args)


def body(rhs_field, panel_inverse, coupling):
    planes = lax.axis_size("plane")
    layers = lax.axis_size("layer")
    place = lax.axis_index("layer")
    plane = lax.axis_index("plane")
    pairs = layers // 2

    block = rhs_field[0]
    parts, loads, ys, chunk = block.shape
    block = block.reshape(parts, loads, planes, ys // planes, chunk)
    block = jnp.moveaxis(block, 2, 0)
    block = lax.all_to_all(block, "plane", split_axis=0, concat_axis=0, tiled=True)
    lines = jnp.moveaxis(block, 0, 3).reshape(parts, loads * ys // planes, planes * chunk)
    shape = lines.shape

    inverse = panel_inverse[0]
    width = inverse.shape[0]
    factors = jnp.broadcast_to(coupling[0].reshape(parts, shape[1], 1), shape)
    down = [(2 * j + 1, 2 * j) for j in range(pairs)]

    rows = width // planes
    piece = lax.dynamic_slice_in_dim(inverse, plane * rows, rows, 0)
    own_piece = piece
    piece = lax.ppermute(piece, "layer", down)
    inverse_next = lax.all_gather(piece, "plane", axis=0, tiled=True)
    lines_next = lax.ppermute(lines, "layer", down)
    factors_next = lax.ppermute(factors, "layer", down)
    quads = layers // 4
    gather = [(4 * j + 2, 4 * j) for j in range(quads)]
    quad_factors = [lax.ppermute(factor, "layer", gather) for factor in (factors, factors_next)]
    last = layers - 4
    quad_lines = [lax.ppermute(source, "layer", [(last + 2, last)]) for source in (lines, lines_next)]

    zero = jnp.zeros(shape, jnp.float32)
    outgoing = jnp.zeros(shape, jnp.bfloat16)
    store_a, store_b = zero, zero
    for panel in range(2):
        if panel > 0:
            incoming = lax.ppermute(outgoing, "layer", [(panel - 1, panel)])
        else:
            incoming = outgoing

        def active(incoming, store_a, outgoing):
            kernel = lambda *refs: forward_kernel(True, *refs)
            return pair_call(kernel, (incoming, lines, factors, inverse), shape, width, 1, 1, 2)

        def idle(incoming, store_a, outgoing):
            return store_a, outgoing

        store_a, outgoing = lax.cond(place == panel, active, idle, incoming, store_a, outgoing)
    store_b = lax.ppermute(store_a, "layer", [(1, 0)])

    for section in range(1, pairs - 2):
        source = 1 if section == 1 else 2 * section - 2
        incoming = lax.ppermute(outgoing, "layer", [(source, 2 * section)])

        def active(incoming, store_a, store_b, outgoing):
            kernel = lambda *refs: forward_kernel(False, *refs)
            args = (incoming, lines, factors, lines_next, factors_next, inverse, inverse_next)
            return pair_call(kernel, args, shape, width, 2, 2, 3)

        def idle(incoming, store_a, store_b, outgoing):
            return store_a, store_b, outgoing

        store_a, store_b, outgoing = lax.cond(
            place == 2 * section, active, idle, incoming, store_a, store_b, outgoing)
        if section == min(7, pairs - 1):
            outgoing, moved = lax.optimization_barrier((outgoing, own_piece))
            quad_inverses = [
                lax.all_gather(lax.ppermute(moved, "layer", [(4 * j + offset, 4 * j) for j in range(quads)]),
                               "plane", axis=0, tiled=True)
                for offset in (2, 3)]

    incoming = lax.ppermute(outgoing, "layer", [(last - 2, last)])

    def active(incoming, store_a, store_b, extra_a, extra_b):
        args = ((incoming, lines, lines_next) + tuple(quad_lines) + (factors, factors_next)
                + tuple(quad_factors) + (inverse, inverse_next) + tuple(quad_inverses))
        return quad_forward_call(args, shape, width)

    def idle(incoming, store_a, store_b, extra_a, extra_b):
        return store_a, store_b, extra_a, extra_b

    store_a, store_b, extra_a, extra_b = lax.cond(
        place == last, active, idle, incoming, store_a, store_b, zero, zero)
    outgoing = jnp.zeros(shape, jnp.bfloat16)
    gather_stores = [(4 * j + 2, 4 * j) for j in range(quads - 1)]
    quad_stores = [jnp.where(place == last, extra, lax.ppermute(store, "layer", gather_stores))
                   for extra, store in ((extra_a, store_a), (extra_b, store_b))]

    sweeps = (zero, zero, zero, zero)
    for section in range(quads):
        lead = layers - 4 - 4 * section
        if section > 0:
            incoming = lax.ppermute(outgoing, "layer", [(lead + 4, lead)])
        else:
            incoming = outgoing

        def active(incoming, sweeps, outgoing, skip=(section == 0)):
            args = ((incoming, store_a, store_b) + tuple(quad_stores) + (factors, factors_next)
                    + tuple(quad_factors) + (inverse, inverse_next) + tuple(quad_inverses))
            results = quad_call(skip, args, shape, width)
            return tuple(results[:4]), results[4]

        def idle(incoming, sweeps, outgoing):
            return sweeps, outgoing

        sweeps, outgoing = lax.cond(place == lead, active, idle, incoming, sweeps, outgoing)

    result = sweeps[0]
    for offset in (1, 2, 3):
        returned = lax.ppermute(sweeps[offset], "layer", [(4 * j, 4 * j + offset) for j in range(quads)])
        result = jnp.where(place % 4 == offset, returned, result)

    result = result.reshape(parts, loads, ys // planes, planes, chunk)
    result = jnp.moveaxis(result, 3, 0)
    result = lax.all_to_all(result, "plane", split_axis=0, concat_axis=0, tiled=True)
    result = jnp.moveaxis(result, 0, 2).reshape(parts, loads, ys, chunk)
    return result[None]


def solution(mesh):
    in_specs = (
        P("layer", None, None, None, "plane"),
        P("layer", None, None),
        P("layer", None, None, "plane"),
    )
    out_specs = P("layer", None, None, None, "plane")
    return jax.shard_map(body, mesh=mesh, in_specs=in_specs, out_specs=out_specs, check_vma=False)
```

```python
import jax
import jax.numpy as jnp
from jax import lax
from jax.experimental import pallas as pl
from jax.experimental.pallas import tpu as pltpu
from jax.sharding import PartitionSpec as P


def kernel_mix(source, factor, carried):
    real = source[0] + (factor[0] * carried[0] - factor[1] * carried[1])
    imag = source[1] + (factor[0] * carried[1] + factor[1] * carried[0])
    return real.astype(jnp.bfloat16), imag.astype(jnp.bfloat16)


def kernel_twist(factor, field):
    real = factor[0] * field[0] - factor[1] * field[1]
    imag = factor[0] * field[1] + factor[1] * field[0]
    return real.astype(jnp.bfloat16), imag.astype(jnp.bfloat16)


def product_into(rows, inverse, out, base=None):
    count = rows[0].shape[0]
    width = inverse.shape[0]
    part = 512
    flat = jnp.concatenate(rows, axis=0)

    def chunk(index, carry):
        low = pl.multiple_of(index * part, part)
        high = pl.multiple_of(width + index * part, part)
        left = jnp.dot(flat, inverse[:, pl.ds(low, part)], preferred_element_type=jnp.float32)
        right = jnp.dot(flat, inverse[:, pl.ds(high, part)], preferred_element_type=jnp.float32)
        real = left[:count] - right[count:]
        imag = right[:count] + left[count:]
        if base is not None:
            real = base[0, :, pl.ds(low, part)] + real
            imag = base[1, :, pl.ds(low, part)] + imag
        out[0, :, pl.ds(low, part)] = real
        out[1, :, pl.ds(low, part)] = imag
        return carry

    lax.fori_loop(0, width // part, chunk, 0)
    return read(out)


def read(ref):
    return ref[0], ref[1]


def write(ref, pair):
    ref[0] = pair[0]
    ref[1] = pair[1]


def widen(pair):
    return tuple(part.astype(jnp.bfloat16).astype(jnp.float32) for part in pair)


def forward_kernel(single, *refs):
    if single:
        incoming, source, factor, inverse, first_out, outgoing, held, sems = refs
    else:
        (incoming, source, factor, source_next, factor_next, inverse, inverse_next,
         first_out, second_out, outgoing, held, sems) = refs
    copies = [pltpu.make_async_copy(inverse, held.at[0], sems.at[0])]
    if not single:
        copies.append(pltpu.make_async_copy(inverse_next, held.at[1], sems.at[1]))
    for copy in copies:
        copy.start()
    carried = tuple(part.astype(jnp.float32) for part in read(incoming))
    mixed = kernel_mix(read(source), read(factor), carried)
    copies[0].wait()
    first = product_into(mixed, held.at[0], first_out)
    if single:
        write(outgoing, tuple(part.astype(jnp.bfloat16) for part in first))
        return
    mixed = kernel_mix(read(source_next), read(factor_next), widen(first))
    copies[1].wait()
    second = product_into(mixed, held.at[1], second_out)
    write(outgoing, tuple(part.astype(jnp.bfloat16) for part in second))


def quad_forward_kernel(incoming, *refs):
    sources, factors, inverses = refs[0:4], refs[4:8], refs[8:12]
    stores, held, sems = refs[12:16], refs[16], refs[17]
    copies = [pltpu.make_async_copy(inverses[i], held.at[i], sems.at[i]) for i in range(4)]
    for panel in range(2):
        copies[panel].start()
    carried = tuple(part.astype(jnp.float32) for part in read(incoming))
    for panel in range(4):
        mixed = kernel_mix(read(sources[panel]), read(factors[panel]), carried)
        copies[panel].wait()
        if panel + 2 < 4:
            copies[panel + 2].start()
        result = product_into(mixed, held.at[panel], stores[panel])
        carried = widen(result)


def quad_forward_call(args, shape, width):
    local = pl.BlockSpec(memory_space=pltpu.VMEM)
    remote = pl.BlockSpec(memory_space=pl.ANY)
    rows = 2 * shape[0] * shape[1]
    return pl.pallas_call(
        quad_forward_kernel,
        out_shape=tuple([jax.ShapeDtypeStruct(shape, jnp.float32)] * 4),
        in_specs=[local] * 9 + [remote] * 4,
        out_specs=tuple([local] * 4),
        scratch_shapes=[pltpu.VMEM((4, width, 2 * width), jnp.bfloat16),
                        pltpu.SemaphoreType.DMA((4,))],
        compiler_params=pltpu.CompilerParams(vmem_limit_bytes=56 * 1024 * 1024),
        cost_estimate=pl.CostEstimate(
            flops=4 * 2 * rows * width * 2 * width, transcendentals=0,
            bytes_accessed=4 * width * 2 * width * 2 + 13 * rows * width * 4),
    )(*args)


def quad_kernel(skip, incoming, *refs):
    stores, factors, inverses = refs[0:4], refs[4:8], refs[8:12]
    sweeps, outgoing, held, sems = refs[12:16], refs[16], refs[17], refs[18]
    order = [2, 1, 0] if skip else [3, 2, 1, 0]
    copies = {i: pltpu.make_async_copy(inverses[i], held.at[i], sems.at[i]) for i in order}
    for panel in order[:2]:
        copies[panel].start()
    queued = 2
    carried = read(incoming)
    for panel in (3, 2, 1, 0):
        if skip and panel == 3:
            sweep = read(stores[panel])
            write(sweeps[panel], sweep)
        else:
            copies[panel].wait()
            if queued < len(order):
                copies[order[queued]].start()
                queued += 1
            sweep = product_into(carried, held.at[panel], sweeps[panel], stores[panel])
        carried = kernel_twist(read(factors[panel]), sweep)
    write(outgoing, carried)


def quad_call(skip, args, shape, width):
    local = pl.BlockSpec(memory_space=pltpu.VMEM)
    remote = pl.BlockSpec(memory_space=pl.ANY)
    rows = 2 * shape[0] * shape[1]
    matmuls = 3 if skip else 4
    out_shape = [jax.ShapeDtypeStruct(shape, jnp.float32)] * 4
    out_shape.append(jax.ShapeDtypeStruct(shape, jnp.bfloat16))
    return pl.pallas_call(
        lambda *refs: quad_kernel(skip, *refs),
        out_shape=tuple(out_shape),
        in_specs=[local] * 9 + [remote] * 4,
        out_specs=tuple([local] * 5),
        scratch_shapes=[pltpu.VMEM((4, width, 2 * width), jnp.bfloat16),
                        pltpu.SemaphoreType.DMA((4,))],
        compiler_params=pltpu.CompilerParams(vmem_limit_bytes=56 * 1024 * 1024),
        cost_estimate=pl.CostEstimate(
            flops=matmuls * 2 * rows * width * 2 * width, transcendentals=0,
            bytes_accessed=matmuls * width * 2 * width * 2 + 14 * rows * width * 4),
    )(*args)


def pair_call(kernel, args, shape, width, matmuls, remotes, results):
    local = pl.BlockSpec(memory_space=pltpu.VMEM)
    remote = pl.BlockSpec(memory_space=pl.ANY)
    rows = 2 * shape[0] * shape[1]
    out_shape = [jax.ShapeDtypeStruct(shape, jnp.float32)] * (results - 1)
    out_shape.append(jax.ShapeDtypeStruct(shape, jnp.bfloat16))
    return pl.pallas_call(
        kernel,
        out_shape=tuple(out_shape),
        in_specs=[local] * (len(args) - remotes) + [remote] * remotes,
        out_specs=tuple([local] * results),
        scratch_shapes=[pltpu.VMEM((2, width, 2 * width), jnp.bfloat16),
                        pltpu.SemaphoreType.DMA((2,))],
        compiler_params=pltpu.CompilerParams(vmem_limit_bytes=48 * 1024 * 1024),
        cost_estimate=pl.CostEstimate(
            flops=matmuls * 2 * rows * width * 2 * width, transcendentals=0,
            bytes_accessed=matmuls * width * 2 * width * 2 + 8 * rows * width * 4),
    )(*args)


def body(rhs_field, panel_inverse, coupling):
    planes = lax.axis_size("plane")
    layers = lax.axis_size("layer")
    place = lax.axis_index("layer")
    plane = lax.axis_index("plane")
    pairs = layers // 2

    block = rhs_field[0]
    parts, loads, ys, chunk = block.shape
    block = block.reshape(parts, loads, planes, ys // planes, chunk)
    block = jnp.moveaxis(block, 2, 0)
    block = lax.all_to_all(block, "plane", split_axis=0, concat_axis=0, tiled=True)
    lines = jnp.moveaxis(block, 0, 3).reshape(parts, loads * ys // planes, planes * chunk)
    shape = lines.shape

    inverse = panel_inverse[0]
    width = inverse.shape[0]
    factors = jnp.broadcast_to(coupling[0].reshape(parts, shape[1], 1), shape)
    down = [(2 * j + 1, 2 * j) for j in range(pairs)]

    rows = width // planes
    piece = lax.dynamic_slice_in_dim(inverse, plane * rows, rows, 0)
    own_piece = piece
    piece = lax.ppermute(piece, "layer", down)
    inverse_next = lax.all_gather(piece, "plane", axis=0, tiled=True)
    lines_next = lax.ppermute(lines, "layer", down)
    factors_next = lax.ppermute(factors, "layer", down)
    quads = layers // 4
    gather = [(4 * j + 2, 4 * j) for j in range(quads)]
    quad_factors = [lax.ppermute(factor, "layer", gather) for factor in (factors, factors_next)]
    last = layers - 4
    quad_lines = [lax.ppermute(source, "layer", [(last + 2, last)]) for source in (lines, lines_next)]

    zero = jnp.zeros(shape, jnp.float32)
    outgoing = jnp.zeros(shape, jnp.bfloat16)
    store_a, store_b = zero, zero
    for panel in range(2):
        if panel > 0:
            incoming = lax.ppermute(outgoing, "layer", [(panel - 1, panel)])
        else:
            incoming = outgoing

        def active(incoming, store_a, outgoing):
            kernel = lambda *refs: forward_kernel(True, *refs)
            return pair_call(kernel, (incoming, lines, factors, inverse), shape, width, 1, 1, 2)

        def idle(incoming, store_a, outgoing):
            return store_a, outgoing

        store_a, outgoing = lax.cond(place == panel, active, idle, incoming, store_a, outgoing)
    store_b = lax.ppermute(store_a, "layer", [(1, 0)])

    for section in range(1, pairs - 2):
        source = 1 if section == 1 else 2 * section - 2
        incoming = lax.ppermute(outgoing, "layer", [(source, 2 * section)])

        def active(incoming, store_a, store_b, outgoing):
            kernel = lambda *refs: forward_kernel(False, *refs)
            args = (incoming, lines, factors, lines_next, factors_next, inverse, inverse_next)
            return pair_call(kernel, args, shape, width, 2, 2, 3)

        def idle(incoming, store_a, store_b, outgoing):
            return store_a, store_b, outgoing

        store_a, store_b, outgoing = lax.cond(
            place == 2 * section, active, idle, incoming, store_a, store_b, outgoing)
        if section == min(7, pairs - 1):
            outgoing, moved = lax.optimization_barrier((outgoing, own_piece))
            quad_inverses = [
                lax.all_gather(lax.ppermute(moved, "layer", [(4 * j + offset, 4 * j) for j in range(quads)]),
                               "plane", axis=0, tiled=True)
                for offset in (2, 3)]

    incoming = lax.ppermute(outgoing, "layer", [(last - 2, last)])

    def active(incoming, store_a, store_b, extra_a, extra_b):
        args = ((incoming, lines, lines_next) + tuple(quad_lines) + (factors, factors_next)
                + tuple(quad_factors) + (inverse, inverse_next) + tuple(quad_inverses))
        return quad_forward_call(args, shape, width)

    def idle(incoming, store_a, store_b, extra_a, extra_b):
        return store_a, store_b, extra_a, extra_b

    store_a, store_b, extra_a, extra_b = lax.cond(
        place == last, active, idle, incoming, store_a, store_b, zero, zero)
    outgoing = jnp.zeros(shape, jnp.bfloat16)
    gather_stores = [(4 * j + 2, 4 * j) for j in range(quads - 1)]
    quad_stores = [jnp.where(place == last, extra, lax.ppermute(store, "layer", gather_stores))
                   for extra, store in ((extra_a, store_a), (extra_b, store_b))]

    sweeps = (zero, zero, zero, zero)
    for section in range(quads):
        lead = layers - 4 - 4 * section
        if section > 0:
            incoming = lax.ppermute(outgoing, "layer", [(lead + 4, lead)])
        else:
            incoming = outgoing

        def active(incoming, sweeps, outgoing, skip=(section == 0)):
            args = ((incoming, store_a, store_b) + tuple(quad_stores) + (factors, factors_next)
                    + tuple(quad_factors) + (inverse, inverse_next) + tuple(quad_inverses))
            results = quad_call(skip, args, shape, width)
            return tuple(results[:4]), results[4]

        def idle(incoming, sweeps, outgoing):
            return sweeps, outgoing

        sweeps, outgoing = lax.cond(place == lead, active, idle, incoming, sweeps, outgoing)

    result = sweeps[0]
    for offset in (1, 2, 3):
        returned = lax.ppermute(sweeps[offset], "layer", [(4 * j, 4 * j + offset) for j in range(quads)])
        result = jnp.where(place % 4 == offset, returned, result)

    result = result.reshape(parts, loads, ys // planes, planes, chunk)
    result = jnp.moveaxis(result, 3, 0)
    result = lax.all_to_all(result, "plane", split_axis=0, concat_axis=0, tiled=True)
    result = jnp.moveaxis(result, 0, 2).reshape(parts, loads, ys, chunk)
    return result[None]


def solution(mesh):
    in_specs = (
        P("layer", None, None, None, "plane"),
        P("layer", None, None),
        P("layer", None, None, "plane"),
    )
    out_specs = P("layer", None, None, None, "plane")
    return jax.shard_map(body, mesh=mesh, in_specs=in_specs, out_specs=out_specs, check_vma=False)
```

```python
import jax
import jax.numpy as jnp
from jax import lax
from jax.experimental import pallas as pl
from jax.experimental.pallas import tpu as pltpu
from jax.sharding import PartitionSpec as P


def kernel_mix(source, factor, carried):
    real = source[0] + (factor[0] * carried[0] - factor[1] * carried[1])
    imag = source[1] + (factor[0] * carried[1] + factor[1] * carried[0])
    return real.astype(jnp.bfloat16), imag.astype(jnp.bfloat16)


def kernel_twist(factor, field):
    real = factor[0] * field[0] - factor[1] * field[1]
    imag = factor[0] * field[1] + factor[1] * field[0]
    return real.astype(jnp.bfloat16), imag.astype(jnp.bfloat16)


def product_into(rows, inverse, out, base=None):
    count = rows[0].shape[0]
    width = inverse.shape[0]
    part = 512
    flat = jnp.concatenate(rows, axis=0)

    def chunk(index, carry):
        low = pl.multiple_of(index * part, part)
        high = pl.multiple_of(width + index * part, part)
        left = jnp.dot(flat, inverse[:, pl.ds(low, part)], preferred_element_type=jnp.float32)
        right = jnp.dot(flat, inverse[:, pl.ds(high, part)], preferred_element_type=jnp.float32)
        real = left[:count] - right[count:]
        imag = right[:count] + left[count:]
        if base is not None:
            real = base[0, :, pl.ds(low, part)] + real
            imag = base[1, :, pl.ds(low, part)] + imag
        out[0, :, pl.ds(low, part)] = real
        out[1, :, pl.ds(low, part)] = imag
        return carry

    lax.fori_loop(0, width // part, chunk, 0)
    return read(out)


def read(ref):
    return ref[0], ref[1]


def write(ref, pair):
    ref[0] = pair[0]
    ref[1] = pair[1]


def widen(pair):
    return tuple(part.astype(jnp.bfloat16).astype(jnp.float32) for part in pair)


def forward_kernel(single, *refs):
    if single:
        incoming, source, factor, inverse, first_out, outgoing, held, sems = refs
    else:
        (incoming, source, factor, source_next, factor_next, inverse, inverse_next,
         first_out, second_out, outgoing, held, sems) = refs
    copies = [pltpu.make_async_copy(inverse, held.at[0], sems.at[0])]
    if not single:
        copies.append(pltpu.make_async_copy(inverse_next, held.at[1], sems.at[1]))
    for copy in copies:
        copy.start()
    carried = tuple(part.astype(jnp.float32) for part in read(incoming))
    mixed = kernel_mix(read(source), read(factor), carried)
    copies[0].wait()
    first = product_into(mixed, held.at[0], first_out)
    if single:
        write(outgoing, tuple(part.astype(jnp.bfloat16) for part in first))
        return
    mixed = kernel_mix(read(source_next), read(factor_next), widen(first))
    copies[1].wait()
    second = product_into(mixed, held.at[1], second_out)
    write(outgoing, tuple(part.astype(jnp.bfloat16) for part in second))


def quad_forward_kernel(incoming, *refs):
    sources, factors, inverses = refs[0:4], refs[4:8], refs[8:12]
    stores, held, sems = refs[12:16], refs[16], refs[17]
    copies = [pltpu.make_async_copy(inverses[i], held.at[i], sems.at[i]) for i in range(4)]
    for panel in range(3):
        copies[panel].start()
    carried = tuple(part.astype(jnp.float32) for part in read(incoming))
    for panel in range(4):
        mixed = kernel_mix(read(sources[panel]), read(factors[panel]), carried)
        copies[panel].wait()
        if panel + 3 < 4:
            copies[panel + 3].start()
        result = product_into(mixed, held.at[panel], stores[panel])
        carried = widen(result)


def quad_forward_call(args, shape, width):
    local = pl.BlockSpec(memory_space=pltpu.VMEM)
    remote = pl.BlockSpec(memory_space=pl.ANY)
    rows = 2 * shape[0] * shape[1]
    return pl.pallas_call(
        quad_forward_kernel,
        out_shape=tuple([jax.ShapeDtypeStruct(shape, jnp.float32)] * 4),
        in_specs=[local] * 9 + [remote] * 4,
        out_specs=tuple([local] * 4),
        scratch_shapes=[pltpu.VMEM((4, width, 2 * width), jnp.bfloat16),
                        pltpu.SemaphoreType.DMA((4,))],
        compiler_params=pltpu.CompilerParams(vmem_limit_bytes=56 * 1024 * 1024),
        cost_estimate=pl.CostEstimate(
            flops=4 * 2 * rows * width * 2 * width, transcendentals=0,
            bytes_accessed=4 * width * 2 * width * 2 + 13 * rows * width * 4),
    )(*args)


def quad_kernel(skip, incoming, *refs):
    stores, factors, inverses = refs[0:4], refs[4:8], refs[8:12]
    sweeps, outgoing, held, sems = refs[12:16], refs[16], refs[17], refs[18]
    order = [2, 1, 0] if skip else [3, 2, 1, 0]
    copies = {i: pltpu.make_async_copy(inverses[i], held.at[i], sems.at[i]) for i in order}
    for panel in order[:3]:
        copies[panel].start()
    queued = 3
    carried = read(incoming)
    for panel in (3, 2, 1, 0):
        if skip and panel == 3:
            sweep = read(stores[panel])
            write(sweeps[panel], sweep)
        else:
            copies[panel].wait()
            if queued < len(order):
                copies[order[queued]].start()
                queued += 1
            sweep = product_into(carried, held.at[panel], sweeps[panel], stores[panel])
        carried = kernel_twist(read(factors[panel]), sweep)
    write(outgoing, carried)


def quad_call(skip, args, shape, width):
    local = pl.BlockSpec(memory_space=pltpu.VMEM)
    remote = pl.BlockSpec(memory_space=pl.ANY)
    rows = 2 * shape[0] * shape[1]
    matmuls = 3 if skip else 4
    out_shape = [jax.ShapeDtypeStruct(shape, jnp.float32)] * 4
    out_shape.append(jax.ShapeDtypeStruct(shape, jnp.bfloat16))
    return pl.pallas_call(
        lambda *refs: quad_kernel(skip, *refs),
        out_shape=tuple(out_shape),
        in_specs=[local] * 9 + [remote] * 4,
        out_specs=tuple([local] * 5),
        scratch_shapes=[pltpu.VMEM((4, width, 2 * width), jnp.bfloat16),
                        pltpu.SemaphoreType.DMA((4,))],
        compiler_params=pltpu.CompilerParams(vmem_limit_bytes=56 * 1024 * 1024),
        cost_estimate=pl.CostEstimate(
            flops=matmuls * 2 * rows * width * 2 * width, transcendentals=0,
            bytes_accessed=matmuls * width * 2 * width * 2 + 14 * rows * width * 4),
    )(*args)


def pair_call(kernel, args, shape, width, matmuls, remotes, results):
    local = pl.BlockSpec(memory_space=pltpu.VMEM)
    remote = pl.BlockSpec(memory_space=pl.ANY)
    rows = 2 * shape[0] * shape[1]
    out_shape = [jax.ShapeDtypeStruct(shape, jnp.float32)] * (results - 1)
    out_shape.append(jax.ShapeDtypeStruct(shape, jnp.bfloat16))
    return pl.pallas_call(
        kernel,
        out_shape=tuple(out_shape),
        in_specs=[local] * (len(args) - remotes) + [remote] * remotes,
        out_specs=tuple([local] * results),
        scratch_shapes=[pltpu.VMEM((2, width, 2 * width), jnp.bfloat16),
                        pltpu.SemaphoreType.DMA((2,))],
        compiler_params=pltpu.CompilerParams(vmem_limit_bytes=48 * 1024 * 1024),
        cost_estimate=pl.CostEstimate(
            flops=matmuls * 2 * rows * width * 2 * width, transcendentals=0,
            bytes_accessed=matmuls * width * 2 * width * 2 + 8 * rows * width * 4),
    )(*args)


def body(rhs_field, panel_inverse, coupling):
    planes = lax.axis_size("plane")
    layers = lax.axis_size("layer")
    place = lax.axis_index("layer")
    plane = lax.axis_index("plane")
    pairs = layers // 2

    block = rhs_field[0]
    parts, loads, ys, chunk = block.shape
    block = block.reshape(parts, loads, planes, ys // planes, chunk)
    block = jnp.moveaxis(block, 2, 0)
    block = lax.all_to_all(block, "plane", split_axis=0, concat_axis=0, tiled=True)
    lines = jnp.moveaxis(block, 0, 3).reshape(parts, loads * ys // planes, planes * chunk)
    shape = lines.shape

    inverse = panel_inverse[0]
    width = inverse.shape[0]
    factors = jnp.broadcast_to(coupling[0].reshape(parts, shape[1], 1), shape)
    down = [(2 * j + 1, 2 * j) for j in range(pairs)]

    rows = width // planes
    piece = lax.dynamic_slice_in_dim(inverse, plane * rows, rows, 0)
    own_piece = piece
    piece = lax.ppermute(piece, "layer", down)
    inverse_next = lax.all_gather(piece, "plane", axis=0, tiled=True)
    lines_next = lax.ppermute(lines, "layer", down)
    factors_next = lax.ppermute(factors, "layer", down)
    quads = layers // 4
    gather = [(4 * j + 2, 4 * j) for j in range(quads)]
    quad_factors = [lax.ppermute(factor, "layer", gather) for factor in (factors, factors_next)]
    last = layers - 4
    quad_lines = [lax.ppermute(source, "layer", [(last + 2, last)]) for source in (lines, lines_next)]

    zero = jnp.zeros(shape, jnp.float32)
    outgoing = jnp.zeros(shape, jnp.bfloat16)
    store_a, store_b = zero, zero
    for panel in range(2):
        if panel > 0:
            incoming = lax.ppermute(outgoing, "layer", [(panel - 1, panel)])
        else:
            incoming = outgoing

        def active(incoming, store_a, outgoing):
            kernel = lambda *refs: forward_kernel(True, *refs)
            return pair_call(kernel, (incoming, lines, factors, inverse), shape, width, 1, 1, 2)

        def idle(incoming, store_a, outgoing):
            return store_a, outgoing

        store_a, outgoing = lax.cond(place == panel, active, idle, incoming, store_a, outgoing)
    store_b = lax.ppermute(store_a, "layer", [(1, 0)])

    for section in range(1, pairs - 2):
        source = 1 if section == 1 else 2 * section - 2
        incoming = lax.ppermute(outgoing, "layer", [(source, 2 * section)])

        def active(incoming, store_a, store_b, outgoing):
            kernel = lambda *refs: forward_kernel(False, *refs)
            args = (incoming, lines, factors, lines_next, factors_next, inverse, inverse_next)
            return pair_call(kernel, args, shape, width, 2, 2, 3)

        def idle(incoming, store_a, store_b, outgoing):
            return store_a, store_b, outgoing

        store_a, store_b, outgoing = lax.cond(
            place == 2 * section, active, idle, incoming, store_a, store_b, outgoing)
        if section == min(7, pairs - 1):
            outgoing, moved = lax.optimization_barrier((outgoing, own_piece))
            quad_inverses = [
                lax.all_gather(lax.ppermute(moved, "layer", [(4 * j + offset, 4 * j) for j in range(quads)]),
                               "plane", axis=0, tiled=True)
                for offset in (2, 3)]

    incoming = lax.ppermute(outgoing, "layer", [(last - 2, last)])

    def active(incoming, store_a, store_b, extra_a, extra_b):
        args = ((incoming, lines, lines_next) + tuple(quad_lines) + (factors, factors_next)
                + tuple(quad_factors) + (inverse, inverse_next) + tuple(quad_inverses))
        return quad_forward_call(args, shape, width)

    def idle(incoming, store_a, store_b, extra_a, extra_b):
        return store_a, store_b, extra_a, extra_b

    store_a, store_b, extra_a, extra_b = lax.cond(
        place == last, active, idle, incoming, store_a, store_b, zero, zero)
    outgoing = jnp.zeros(shape, jnp.bfloat16)
    gather_stores = [(4 * j + 2, 4 * j) for j in range(quads - 1)]
    quad_stores = [jnp.where(place == last, extra, lax.ppermute(store, "layer", gather_stores))
                   for extra, store in ((extra_a, store_a), (extra_b, store_b))]

    sweeps = (zero, zero, zero, zero)
    for section in range(quads):
        lead = layers - 4 - 4 * section
        if section > 0:
            incoming = lax.ppermute(outgoing, "layer", [(lead + 4, lead)])
        else:
            incoming = outgoing

        def active(incoming, sweeps, outgoing, skip=(section == 0)):
            args = ((incoming, store_a, store_b) + tuple(quad_stores) + (factors, factors_next)
                    + tuple(quad_factors) + (inverse, inverse_next) + tuple(quad_inverses))
            results = quad_call(skip, args, shape, width)
            return tuple(results[:4]), results[4]

        def idle(incoming, sweeps, outgoing):
            return sweeps, outgoing

        sweeps, outgoing = lax.cond(place == lead, active, idle, incoming, sweeps, outgoing)

    result = sweeps[0]
    for offset in (1, 2, 3):
        returned = lax.ppermute(sweeps[offset], "layer", [(4 * j, 4 * j + offset) for j in range(quads)])
        result = jnp.where(place % 4 == offset, returned, result)

    result = result.reshape(parts, loads, ys // planes, planes, chunk)
    result = jnp.moveaxis(result, 3, 0)
    result = lax.all_to_all(result, "plane", split_axis=0, concat_axis=0, tiled=True)
    result = jnp.moveaxis(result, 0, 2).reshape(parts, loads, ys, chunk)
    return result[None]


def solution(mesh):
    in_specs = (
        P("layer", None, None, None, "plane"),
        P("layer", None, None),
        P("layer", None, None, "plane"),
    )
    out_specs = P("layer", None, None, None, "plane")
    return jax.shard_map(body, mesh=mesh, in_specs=in_specs, out_specs=out_specs, check_vma=False)
```

```python
import jax
import jax.numpy as jnp
from jax import lax
from jax.experimental import pallas as pl
from jax.experimental.pallas import tpu as pltpu
from jax.sharding import PartitionSpec as P


def kernel_mix(source, factor, carried):
    real = source[0] + (factor[0] * carried[0] - factor[1] * carried[1])
    imag = source[1] + (factor[0] * carried[1] + factor[1] * carried[0])
    return real.astype(jnp.bfloat16), imag.astype(jnp.bfloat16)


def kernel_twist(factor, field):
    real = factor[0] * field[0] - factor[1] * field[1]
    imag = factor[0] * field[1] + factor[1] * field[0]
    return real.astype(jnp.bfloat16), imag.astype(jnp.bfloat16)


def product_into(rows, inverse, out, base=None):
    count = rows[0].shape[0]
    width = inverse.shape[0]
    part = 512
    flat = jnp.concatenate(rows, axis=0)

    def chunk(index, carry):
        low = pl.multiple_of(index * part, part)
        high = pl.multiple_of(width + index * part, part)
        left = jnp.dot(flat, inverse[:, pl.ds(low, part)], preferred_element_type=jnp.float32)
        right = jnp.dot(flat, inverse[:, pl.ds(high, part)], preferred_element_type=jnp.float32)
        real = left[:count] - right[count:]
        imag = right[:count] + left[count:]
        if base is not None:
            real = base[0, :, pl.ds(low, part)] + real
            imag = base[1, :, pl.ds(low, part)] + imag
        out[0, :, pl.ds(low, part)] = real
        out[1, :, pl.ds(low, part)] = imag
        return carry

    lax.fori_loop(0, width // part, chunk, 0)
    return read(out)


def read(ref):
    return ref[0], ref[1]


def write(ref, pair):
    ref[0] = pair[0]
    ref[1] = pair[1]


def widen(pair):
    return tuple(part.astype(jnp.bfloat16).astype(jnp.float32) for part in pair)


def half_copies(inverse, slot, sems):
    width = inverse.shape[0]
    return [pltpu.make_async_copy(inverse.at[:, pl.ds(half * width, width)],
                                  slot.at[:, pl.ds(half * width, width)], sems.at[half])
            for half in range(2)]


def forward_kernel(single, *refs):
    if single:
        incoming, source, factor, inverse, first_out, outgoing, held, sems = refs
    else:
        (incoming, source, factor, source_next, factor_next, inverse, inverse_next,
         first_out, second_out, outgoing, held, sems) = refs
    first_copies = half_copies(inverse, held.at[0], sems.at[0])
    for copy in first_copies:
        copy.start()
    carried = tuple(part.astype(jnp.float32) for part in read(incoming))
    mixed = kernel_mix(read(source), read(factor), carried)
    for copy in first_copies:
        copy.wait()
    if not single:
        second_copies = half_copies(inverse_next, held.at[1], sems.at[1])
        for copy in second_copies:
            copy.start()
    first = product_into(mixed, held.at[0], first_out)
    if single:
        write(outgoing, tuple(part.astype(jnp.bfloat16) for part in first))
        return
    mixed = kernel_mix(read(source_next), read(factor_next), widen(first))
    for copy in second_copies:
        copy.wait()
    second = product_into(mixed, held.at[1], second_out)
    write(outgoing, tuple(part.astype(jnp.bfloat16) for part in second))


def quad_forward_kernel(incoming, *refs):
    sources, factors, inverses = refs[0:4], refs[4:8], refs[8:12]
    stores, held, sems = refs[12:16], refs[16], refs[17]
    copies = [pltpu.make_async_copy(inverses[i], held.at[i], sems.at[i]) for i in range(4)]
    for panel in range(2):
        copies[panel].start()
    carried = tuple(part.astype(jnp.float32) for part in read(incoming))
    for panel in range(4):
        mixed = kernel_mix(read(sources[panel]), read(factors[panel]), carried)
        copies[panel].wait()
        if panel + 2 < 4:
            copies[panel + 2].start()
        result = product_into(mixed, held.at[panel], stores[panel])
        carried = widen(result)


def quad_forward_call(args, shape, width):
    local = pl.BlockSpec(memory_space=pltpu.VMEM)
    remote = pl.BlockSpec(memory_space=pl.ANY)
    rows = 2 * shape[0] * shape[1]
    return pl.pallas_call(
        quad_forward_kernel,
        out_shape=tuple([jax.ShapeDtypeStruct(shape, jnp.float32)] * 4),
        in_specs=[local] * 9 + [remote] * 4,
        out_specs=tuple([local] * 4),
        scratch_shapes=[pltpu.VMEM((4, width, 2 * width), jnp.bfloat16),
                        pltpu.SemaphoreType.DMA((4,))],
        compiler_params=pltpu.CompilerParams(vmem_limit_bytes=56 * 1024 * 1024),
        cost_estimate=pl.CostEstimate(
            flops=4 * 2 * rows * width * 2 * width, transcendentals=0,
            bytes_accessed=4 * width * 2 * width * 2 + 13 * rows * width * 4),
    )(*args)


def quad_kernel(skip, incoming, *refs):
    stores, factors, inverses = refs[0:4], refs[4:8], refs[8:12]
    sweeps, outgoing, held, sems = refs[12:16], refs[16], refs[17], refs[18]
    order = [2, 1, 0] if skip else [3, 2, 1, 0]
    copies = {i: pltpu.make_async_copy(inverses[i], held.at[i], sems.at[i]) for i in order}
    for panel in order[:2]:
        copies[panel].start()
    queued = 2
    carried = read(incoming)
    for panel in (3, 2, 1, 0):
        if skip and panel == 3:
            sweep = read(stores[panel])
            write(sweeps[panel], sweep)
        else:
            copies[panel].wait()
            if queued < len(order):
                copies[order[queued]].start()
                queued += 1
            sweep = product_into(carried, held.at[panel], sweeps[panel], stores[panel])
        carried = kernel_twist(read(factors[panel]), sweep)
    write(outgoing, carried)


def quad_call(skip, args, shape, width):
    local = pl.BlockSpec(memory_space=pltpu.VMEM)
    remote = pl.BlockSpec(memory_space=pl.ANY)
    rows = 2 * shape[0] * shape[1]
    matmuls = 3 if skip else 4
    out_shape = [jax.ShapeDtypeStruct(shape, jnp.float32)] * 4
    out_shape.append(jax.ShapeDtypeStruct(shape, jnp.bfloat16))
    return pl.pallas_call(
        lambda *refs: quad_kernel(skip, *refs),
        out_shape=tuple(out_shape),
        in_specs=[local] * 9 + [remote] * 4,
        out_specs=tuple([local] * 5),
        scratch_shapes=[pltpu.VMEM((4, width, 2 * width), jnp.bfloat16),
                        pltpu.SemaphoreType.DMA((4,))],
        compiler_params=pltpu.CompilerParams(vmem_limit_bytes=56 * 1024 * 1024),
        cost_estimate=pl.CostEstimate(
            flops=matmuls * 2 * rows * width * 2 * width, transcendentals=0,
            bytes_accessed=matmuls * width * 2 * width * 2 + 14 * rows * width * 4),
    )(*args)


def pair_call(kernel, args, shape, width, matmuls, remotes, results):
    local = pl.BlockSpec(memory_space=pltpu.VMEM)
    remote = pl.BlockSpec(memory_space=pl.ANY)
    rows = 2 * shape[0] * shape[1]
    out_shape = [jax.ShapeDtypeStruct(shape, jnp.float32)] * (results - 1)
    out_shape.append(jax.ShapeDtypeStruct(shape, jnp.bfloat16))
    return pl.pallas_call(
        kernel,
        out_shape=tuple(out_shape),
        in_specs=[local] * (len(args) - remotes) + [remote] * remotes,
        out_specs=tuple([local] * results),
        scratch_shapes=[pltpu.VMEM((2, width, 2 * width), jnp.bfloat16),
                        pltpu.SemaphoreType.DMA((2, 2))],
        compiler_params=pltpu.CompilerParams(vmem_limit_bytes=48 * 1024 * 1024),
        cost_estimate=pl.CostEstimate(
            flops=matmuls * 2 * rows * width * 2 * width, transcendentals=0,
            bytes_accessed=matmuls * width * 2 * width * 2 + 8 * rows * width * 4),
    )(*args)


def body(rhs_field, panel_inverse, coupling):
    planes = lax.axis_size("plane")
    layers = lax.axis_size("layer")
    place = lax.axis_index("layer")
    plane = lax.axis_index("plane")
    pairs = layers // 2

    block = rhs_field[0]
    parts, loads, ys, chunk = block.shape
    block = block.reshape(parts, loads, planes, ys // planes, chunk)
    block = jnp.moveaxis(block, 2, 0)
    block = lax.all_to_all(block, "plane", split_axis=0, concat_axis=0, tiled=True)
    lines = jnp.moveaxis(block, 0, 3).reshape(parts, loads * ys // planes, planes * chunk)
    shape = lines.shape

    inverse = panel_inverse[0]
    width = inverse.shape[0]
    factors = jnp.broadcast_to(coupling[0].reshape(parts, shape[1], 1), shape)
    down = [(2 * j + 1, 2 * j) for j in range(pairs)]

    rows = width // planes
    piece = lax.dynamic_slice_in_dim(inverse, plane * rows, rows, 0)
    own_piece = piece
    piece = lax.ppermute(piece, "layer", down)
    inverse_next = lax.all_gather(piece, "plane", axis=0, tiled=True)
    lines_next = lax.ppermute(lines, "layer", down)
    factors_next = lax.ppermute(factors, "layer", down)
    quads = layers // 4
    gather = [(4 * j + 2, 4 * j) for j in range(quads)]
    quad_factors = [lax.ppermute(factor, "layer", gather) for factor in (factors, factors_next)]
    last = layers - 4
    quad_lines = [lax.ppermute(source, "layer", [(last + 2, last)]) for source in (lines, lines_next)]

    zero = jnp.zeros(shape, jnp.float32)
    outgoing = jnp.zeros(shape, jnp.bfloat16)
    store_a, store_b = zero, zero
    for panel in range(2):
        if panel > 0:
            incoming = lax.ppermute(outgoing, "layer", [(panel - 1, panel)])
        else:
            incoming = outgoing

        def active(incoming, store_a, outgoing):
            kernel = lambda *refs: forward_kernel(True, *refs)
            return pair_call(kernel, (incoming, lines, factors, inverse), shape, width, 1, 1, 2)

        def idle(incoming, store_a, outgoing):
            return store_a, outgoing

        store_a, outgoing = lax.cond(place == panel, active, idle, incoming, store_a, outgoing)
    store_b = lax.ppermute(store_a, "layer", [(1, 0)])

    for section in range(1, pairs - 2):
        source = 1 if section == 1 else 2 * section - 2
        incoming = lax.ppermute(outgoing, "layer", [(source, 2 * section)])

        def active(incoming, store_a, store_b, outgoing):
            kernel = lambda *refs: forward_kernel(False, *refs)
            args = (incoming, lines, factors, lines_next, factors_next, inverse, inverse_next)
            return pair_call(kernel, args, shape, width, 2, 2, 3)

        def idle(incoming, store_a, store_b, outgoing):
            return store_a, store_b, outgoing

        store_a, store_b, outgoing = lax.cond(
            place == 2 * section, active, idle, incoming, store_a, store_b, outgoing)
        if section == min(7, pairs - 1):
            outgoing, moved = lax.optimization_barrier((outgoing, own_piece))
            quad_inverses = [
                lax.all_gather(lax.ppermute(moved, "layer", [(4 * j + offset, 4 * j) for j in range(quads)]),
                               "plane", axis=0, tiled=True)
                for offset in (2, 3)]

    incoming = lax.ppermute(outgoing, "layer", [(last - 2, last)])

    def active(incoming, store_a, store_b, extra_a, extra_b):
        args = ((incoming, lines, lines_next) + tuple(quad_lines) + (factors, factors_next)
                + tuple(quad_factors) + (inverse, inverse_next) + tuple(quad_inverses))
        return quad_forward_call(args, shape, width)

    def idle(incoming, store_a, store_b, extra_a, extra_b):
        return store_a, store_b, extra_a, extra_b

    store_a, store_b, extra_a, extra_b = lax.cond(
        place == last, active, idle, incoming, store_a, store_b, zero, zero)
    outgoing = jnp.zeros(shape, jnp.bfloat16)
    gather_stores = [(4 * j + 2, 4 * j) for j in range(quads - 1)]
    quad_stores = [jnp.where(place == last, extra, lax.ppermute(store, "layer", gather_stores))
                   for extra, store in ((extra_a, store_a), (extra_b, store_b))]

    sweeps = (zero, zero, zero, zero)
    for section in range(quads):
        lead = layers - 4 - 4 * section
        if section > 0:
            incoming = lax.ppermute(outgoing, "layer", [(lead + 4, lead)])
        else:
            incoming = outgoing

        def active(incoming, sweeps, outgoing, skip=(section == 0)):
            args = ((incoming, store_a, store_b) + tuple(quad_stores) + (factors, factors_next)
                    + tuple(quad_factors) + (inverse, inverse_next) + tuple(quad_inverses))
            results = quad_call(skip, args, shape, width)
            return tuple(results[:4]), results[4]

        def idle(incoming, sweeps, outgoing):
            return sweeps, outgoing

        sweeps, outgoing = lax.cond(place == lead, active, idle, incoming, sweeps, outgoing)

    result = sweeps[0]
    for offset in (1, 2, 3):
        returned = lax.ppermute(sweeps[offset], "layer", [(4 * j, 4 * j + offset) for j in range(quads)])
        result = jnp.where(place % 4 == offset, returned, result)

    result = result.reshape(parts, loads, ys // planes, planes, chunk)
    result = jnp.moveaxis(result, 3, 0)
    result = lax.all_to_all(result, "plane", split_axis=0, concat_axis=0, tiled=True)
    result = jnp.moveaxis(result, 0, 2).reshape(parts, loads, ys, chunk)
    return result[None]


def solution(mesh):
    in_specs = (
        P("layer", None, None, None, "plane"),
        P("layer", None, None),
        P("layer", None, None, "plane"),
    )
    out_specs = P("layer", None, None, None, "plane")
    return jax.shard_map(body, mesh=mesh, in_specs=in_specs, out_specs=out_specs, check_vma=False)
```
